256 devices in a mesh: tile: 64 (over y_hi, z, x), fsdp: 4 (over y_lo, core).
Axes of the slice: x: 4, y: 4 (y_hi: 2, y_lo: 2; y = y_hi * 2 + y_lo), z: 8, core: 2. Of those that a mesh axis runs over, the one named last changes fastest.
Arguments:
- fields: bfloat16 [4, 32, 512, 512], P('fsdp', None, 'tile'), may hold values from -6 to 6
- seam_shift: int32 [64, 2], P('tile'), may hold values from -4 to 4
- kernel: float32 [49, 512], replicated, may hold values from -0.875 to 0.875
- gain: float32 [512], replicated, may hold values from 0.3 to 3
- w_in: bfloat16 [512, 2048], P(None, 'fsdp'), may hold values from -0.25 to 0.25
- w_out: bfloat16 [2048, 512], P('fsdp'), may hold values from -0.125 to 0.125
- cotangent: bfloat16 [4, 32, 512, 512], P('fsdp', None, 'tile'), may hold values from -6 to 6
Outputs:
- mixed: bfloat16 [4, 32, 512, 512], P('fsdp', None, 'tile')
- field_grad: bfloat16 [4, 32, 512, 512], P('fsdp', None, 'tile')
- kernel_grad: float32 [49, 512], replicated
- gain_grad: float32 [512], replicated
- w_in_grad: float32 [512, 2048], P(None, 'fsdp')
- w_out_grad: float32 [2048, 512], P('fsdp')
The draws below stay inside these ranges and needn't reach their ends.
Inputs may be any that keep to these rules, and one draw needn't show every extreme that they name: `seam_shift`: offset added to the row index of cells taken across a tile's west (column 0) or east (column 1) seam.
All inputs are finite; a program needn't handle non-finite values.
Results may differ from the reference program's by a relative error of at most 0.0095.
Values may be sent and summed in bfloat16 or wider, within the bound.
No kernel may reach another device: no remote copies, remote signals or barrier semaphores. Data moves between devices by JAX's collectives and lax.ppermute only.
A program may use at most 128 MiB of HBM per device.

```python
import math
import jax
import jax.numpy as jnp
from jax import lax

C = 512
HID = 2048
TAPS = 49
LAT = 32
LON_DEV = 8
SAMPLES = 4
TILES = 64
LON = 512
CELLS = 65536


def touch_ends(drawn, stream_key, smallest, largest):
    shape = drawn.shape
    index_at = [jax.random.randint(jax.random.fold_in(stream_key, axis), (), 0, shape[axis]) for axis in range(len(shape))]
    drawn = drawn.at[tuple(index_at)].set(smallest)
    longest = shape.index(max(shape))
    index_at[longest] = (index_at[longest] + 1) % shape[longest]
    return drawn.at[tuple(index_at)].set(largest)


def block_scale(own_key, dims, pieces, low, high):
    level = 1.0
    for axis_at, parts in pieces:
        heights = jax.random.uniform(jax.random.fold_in(jax.random.fold_in(own_key, 6), axis_at), (parts,), jnp.float32, low / len(pieces), high / len(pieces))
        level = level * jnp.repeat(jnp.exp(heights), dims[axis_at] // parts).reshape((-1,) + (1,) * (len(dims) - 1 - axis_at))
    return level


def centred(rng, dims, deviation, most, cuts=(), kind=jnp.bfloat16):
    entries = jax.random.normal(rng, dims, jnp.float32) * deviation
    if len(cuts) > 0:
        entries = block_scale(rng, dims, cuts, -0.22, 0.18) * entries
    return jnp.clip(entries, min=-most, max=most).astype(kind)


def setup_inputs(seed: int = 0) -> dict:
    streams_of = jax.random.split(jax.random.key(seed), 8)
    fields = centred(streams_of[0], (SAMPLES, LAT, LON, C), 1.0, 6.0, ((0, 4), (2, 64)))
    seam_shift = touch_ends(jax.random.randint(streams_of[1], (TILES, 2), -4, 5), jax.random.fold_in(streams_of[1], 1), -4, 4).astype(jnp.int32)
    kernel = centred(streams_of[2], (TAPS, C), TAPS ** -0.5, 0.875, (), jnp.float32)
    gain = jnp.clip(jnp.exp(jax.random.uniform(streams_of[3], (C,), jnp.float32, math.log(0.3), math.log(3.0))), 0.3, 3.0)
    w_in = centred(streams_of[4], (C, HID), C ** -0.5, 0.25, ((1, 4),))
    w_out = centred(streams_of[5], (HID, C), HID ** -0.5, 0.125, ((0, 4),))
    cotangent = centred(streams_of[6], (SAMPLES, LAT, LON, C), 1.0, 6.0, ((0, 4), (2, 64)))
    return dict(fields=fields, seam_shift=seam_shift, kernel=kernel, gain=gain, w_in=w_in, w_out=w_out, cotangent=cotangent)


eps = 1e-06
inv_root2 = 0.7071067811865476
inv_root_tau = 0.3989422804014327

def gelu(value):
    return value * 0.5 * (1.0 + lax.erf(value * inv_root2))

def gelu_slope(value):
    return 0.5 * (1.0 + lax.erf(value * inv_root2)) + value * inv_root_tau * jnp.exp(-0.5 * value * value)

def shift_rows(strip, offsets):
    height = strip.shape[0]
    rows = jnp.arange(height, dtype=jnp.int32)[:, None] + offsets[None, :].astype(jnp.int32)
    valid = (rows >= 0) & (rows < height)
    clipped = jnp.clip(rows, 0, height - 1).astype(jnp.int32)
    index = jnp.broadcast_to(clipped[:, :, None, None], strip.shape)
    taken = jnp.take_along_axis(strip, index, axis=0)
    return jnp.where(valid[:, :, None, None], taken, jnp.zeros_like(taken))

def extend(plane, seam_shift):
    tiles = plane.reshape(LAT, TILES, LON_DEV, C)
    west = shift_rows(jnp.roll(tiles, 1, axis=1)[:, :, LON_DEV - 3:], seam_shift[:, 0])
    east = shift_rows(jnp.roll(tiles, -1, axis=1)[:, :, :3], seam_shift[:, 1])
    joined = jnp.concatenate([west, tiles, east], axis=2)
    return jnp.pad(joined, ((3, 3), (0, 0), (0, 0), (0, 0)))

def depthwise(padded, kernel):
    total = jnp.zeros((LAT, TILES, LON_DEV, C), jnp.float32)
    for row in range(7):
        for col in range(7):
            total = total + padded[row:row + LAT, :, col:col + LON_DEV, :] * kernel[7 * row + col]
    return total

def reference(fields, seam_shift, kernel, gain, w_in, w_out, cotangent):

    def tile_step(carry, inputs):
        sum_in, sum_out, sum_gain = carry
        mixed_tile, plane_tile, back_tile = inputs
        rows = mixed_tile.reshape(LAT * LON_DEV, C)
        mean = lax.optimization_barrier(jnp.mean(rows, axis=-1, keepdims=True))
        centered = rows - mean
        rstd = lax.rsqrt(lax.optimization_barrier(jnp.mean(centered * centered, axis=-1, keepdims=True)) + eps)
        normed = centered * rstd
        scaled = (normed * gain).astype(jnp.bfloat16)
        pre = jnp.dot(scaled, w_in, preferred_element_type=jnp.float32)
        hidden = gelu(pre).astype(jnp.bfloat16)
        branch = jnp.dot(hidden, w_out, preferred_element_type=jnp.float32)
        residual = plane_tile.reshape(LAT * LON_DEV, C).astype(jnp.float32)
        output = (residual + branch).astype(jnp.bfloat16).reshape(LAT, LON_DEV, C)
        back = back_tile.reshape(LAT * LON_DEV, C)
        d_hidden = lax.dot_general(back, w_out, (((1,), (1,)), ((), ())), preferred_element_type=jnp.float32)
        d_pre = (d_hidden * gelu_slope(pre)).astype(jnp.bfloat16)
        term_out = lax.dot_general(hidden, back, (((0,), (0,)), ((), ())), preferred_element_type=jnp.float32)
        term_in = lax.dot_general(scaled, d_pre, (((0,), (0,)), ((), ())), preferred_element_type=jnp.float32)
        d_scaled = lax.dot_general(d_pre, w_in, (((1,), (1,)), ((), ())), preferred_element_type=jnp.float32)
        term_gain = lax.optimization_barrier(jnp.sum(d_scaled * normed, axis=0))
        d_normed = d_scaled * gain
        d_rows = (d_normed - lax.optimization_barrier(jnp.mean(d_normed, axis=-1, keepdims=True)) - normed * lax.optimization_barrier(jnp.mean(d_normed * normed, axis=-1, keepdims=True))) * rstd
        return ((sum_in + term_in, sum_out + term_out, sum_gain + term_gain), (output, d_rows.reshape(LAT, LON_DEV, C)))

    def by_tile(plane):
        return jnp.moveaxis(plane.reshape(LAT, TILES, LON_DEV, C), 1, 0)

    def sample_step(carry, inputs):
        sum_in, sum_out, sum_gain, sum_kernel = carry
        plane, back_plane = inputs
        plane32 = plane.astype(jnp.float32)
        mixed_in, pullback = jax.vjp(lambda field, taps: depthwise(extend(field, seam_shift), taps), plane32, kernel)
        (sum_in, sum_out, sum_gain), (out_tiles, d_tiles) = lax.scan(tile_step, (sum_in, sum_out, sum_gain), (jnp.moveaxis(mixed_in, 1, 0), by_tile(plane), by_tile(back_plane)))
        d_plane, d_kernel = pullback(jnp.moveaxis(d_tiles, 0, 1))
        mixed_plane = jnp.moveaxis(out_tiles, 0, 1).reshape(LAT, LON, C)
        grad_plane = (back_plane.astype(jnp.float32) + d_plane).astype(jnp.bfloat16)
        return ((sum_in, sum_out, sum_gain, sum_kernel + d_kernel), (mixed_plane, grad_plane))
    start = (jnp.zeros((C, HID), jnp.float32), jnp.zeros((HID, C), jnp.float32), jnp.zeros((C,), jnp.float32), jnp.zeros((TAPS, C), jnp.float32))
    (sum_in, sum_out, sum_gain, sum_kernel), (mixed, field_grad) = lax.scan(sample_step, start, (fields, cotangent))
    factor = 1.0 / math.sqrt(CELLS)
    return (mixed, field_grad, sum_kernel * factor, sum_gain * factor, sum_in * factor, sum_out * factor)
```

```python
import math

import jax
import jax.numpy as jnp
from jax import lax
from jax.sharding import PartitionSpec as P

eps = 1e-06
inv_root2 = 0.7071067811865476
inv_root_tau = 0.3989422804014327


def extended(cells, sides, width):
    for axis, dim in sides:
        count = lax.axis_size(axis)
        head = lax.slice_in_dim(cells, 0, width, axis=dim)
        tail = lax.slice_in_dim(cells, cells.shape[dim] - width, cells.shape[dim], axis=dim)
        cells = jnp.concatenate(
            [
                lax.ppermute(tail, axis, [(i, (i + 1) % count) for i in range(count)]),
                cells,
                lax.ppermute(head, axis, [((i + 1) % count, i) for i in range(count)]),
            ],
            axis=dim,
        )
    return cells


def exchange(value, axis, bit):
    count = lax.axis_size(axis)
    return lax.ppermute(value, axis, [(i, i ^ (1 << bit)) for i in range(count)])


def fsdp_summed(stacked):
    me = lax.axis_index("fsdp")
    for bit in (0, 1):
        half = stacked.shape[0] // 2
        side = (me >> bit) & 1
        keep = lax.dynamic_slice_in_dim(stacked, side * half, half, 0).astype(jnp.bfloat16)
        send = lax.dynamic_slice_in_dim(stacked, (1 - side) * half, half, 0).astype(jnp.bfloat16)
        got = exchange(send, "fsdp", bit)
        stacked = keep.astype(jnp.float32) + got.astype(jnp.float32)
    return stacked


def halve(part, me, bit):
    half = part.shape[0] // 2
    side = (me >> bit) & 1
    keep = lax.dynamic_slice_in_dim(part, side * half, half, 0)
    send = lax.dynamic_slice_in_dim(part, (1 - side) * half, half, 0)
    return keep + exchange(send, "tile", bit)


def double(part, me, bit):
    side = (me >> bit) & 1
    got = exchange(part, "tile", bit)
    return jnp.concatenate(
        [jnp.where(side == 0, part, got), jnp.where(side == 0, got, part)], axis=0
    )


def tile_summed(low, high):
    assert lax.axis_size("tile") == 64
    me = lax.axis_index("tile")
    order_low, order_high = (0, 2, 1, 3, 4, 5), (2, 0, 3, 1, 5, 4)
    for a, b in zip(order_low, order_high):
        low, high = halve(low, me, a), halve(high, me, b)
    for a, b in zip(reversed(order_low), reversed(order_high)):
        low, high = double(low, me, a), double(high, me, b)
    return low, high


def gelu(value):
    return value * 0.5 * (1.0 + lax.erf(value * inv_root2))


def gelu_slope(value):
    return 0.5 * (1.0 + lax.erf(value * inv_root2)) + value * inv_root_tau * jnp.exp(
        -0.5 * value * value
    )


def shift_rows(strip, offset):
    height = strip.shape[1]
    wider = jnp.pad(strip, ((0, 0), (height, height), (0, 0), (0, 0)))
    return lax.dynamic_slice_in_dim(wider, height + offset, height, 1)


def depthwise(padded, kernel):
    height = padded.shape[1] - 6
    width = padded.shape[2] - 6
    total = jnp.zeros((padded.shape[0], height, width, padded.shape[3]), jnp.float32)
    for row in range(7):
        for col in range(7):
            total = (
                total + padded[:, row : row + height, col : col + width, :] * kernel[7 * row + col]
            )
    return total


def body(fields, seam_shift, kernel, gain, w_in, w_out, cotangent):
    height = fields.shape[1]
    width = fields.shape[2]
    channels = fields.shape[3]
    count = fields.shape[0] * height * width
    cells = count * lax.axis_size("tile") * lax.axis_size("fsdp")
    factor = 1.0 / math.sqrt(cells)
    west_shift = seam_shift[0, 0]
    east_shift = seam_shift[0, 1]
    row_pad = ((0, 0), (3, 3), (0, 0), (0, 0))
    widened = extended(fields, (("tile", 2),), 3)
    west = shift_rows(widened[:, :, :3], west_shift)
    east = shift_rows(widened[:, :, width + 3 :], east_shift)
    padded = jnp.pad(jnp.concatenate([west, fields, east], axis=2), row_pad)
    mixed_in = depthwise(padded, kernel)
    rows = mixed_in.reshape(count, channels)
    mean = jnp.mean(rows, axis=-1, keepdims=True)
    centered = rows - mean
    rstd = lax.rsqrt(jnp.mean(centered * centered, axis=-1, keepdims=True) + eps)
    normed = centered * rstd
    scaled = (normed * gain).astype(jnp.bfloat16)
    back = cotangent.reshape(count, channels)
    contract_last = (((1,), (1,)), ((), ()))
    full_in, full_out = (
        lax.all_gather(w_in, "fsdp", axis=1, tiled=True),
        lax.all_gather(w_out, "fsdp", axis=0, tiled=True),
    )
    pre = jnp.dot(scaled, full_in, preferred_element_type=jnp.float32)
    hidden = gelu(pre).astype(jnp.bfloat16)
    branch = jnp.dot(hidden, full_out, preferred_element_type=jnp.float32)
    d_hidden = lax.dot_general(back, full_out, contract_last, preferred_element_type=jnp.float32)
    residual = fields.reshape(count, channels).astype(jnp.float32)
    mixed = (residual + branch).astype(jnp.bfloat16).reshape(fields.shape)
    d_pre = (d_hidden * gelu_slope(pre)).astype(jnp.bfloat16)
    d_scaled = lax.dot_general(d_pre, full_in, contract_last, preferred_element_type=jnp.float32)
    term_gain = jnp.sum(d_scaled * normed, axis=0) * factor
    d_normed = d_scaled * gain
    d_rows = (
        d_normed
        - jnp.mean(d_normed, axis=-1, keepdims=True)
        - normed * jnp.mean(d_normed * normed, axis=-1, keepdims=True)
    ) * rstd
    d_mixed = d_rows.reshape(mixed_in.shape)
    unused, pullback = jax.vjp(depthwise, padded.astype(jnp.float32), kernel)
    d_padded, kernel_term = pullback(d_mixed)
    kernel_term = kernel_term * factor
    d_core = d_padded[:, 3 : height + 3]
    d_west = shift_rows(d_core[:, :, :3], -west_shift)
    d_east = shift_rows(d_core[:, :, width + 3 :], -east_shift)
    returned = extended(
        jnp.concatenate([d_west, d_east], axis=2).astype(jnp.bfloat16), (("tile", 2),), 3
    ).astype(jnp.float32)
    own = cotangent.astype(jnp.float32) + d_core[:, :, 3 : width + 3]
    field_grad = jnp.concatenate(
        [
            own[:, :, :3] + returned[:, :, :3],
            own[:, :, 3 : width - 3],
            own[:, :, width - 3 :] + returned[:, :, 9:],
        ],
        axis=2,
    ).astype(jnp.bfloat16)
    parts = lax.axis_size("fsdp")
    assert parts == 4
    share = full_in.shape[1] // parts
    d_pre4 = d_pre.reshape(count, 2, 2, share)
    hidden4 = hidden.reshape(count, 2, 2, share)
    term_in4 = jnp.einsum("ck,cabh->bakh", scaled, d_pre4, preferred_element_type=jnp.float32)
    term_out4 = jnp.einsum("cabh,cj->bahj", hidden4, back, preferred_element_type=jnp.float32)
    spare = -(kernel_term.shape[0] + 1) % 64
    small = jnp.concatenate(
        [kernel_term, term_gain[None], jnp.zeros((spare, channels), jnp.float32)], axis=0
    )
    small4 = jnp.broadcast_to(small, (2, 2) + small.shape)
    stacked = jnp.concatenate(
        [
            (term_in4 * factor).astype(jnp.bfloat16),
            small4.astype(jnp.bfloat16),
            (term_out4 * factor).astype(jnp.bfloat16),
        ],
        axis=2,
    ).reshape(-1, channels)
    chunk = fsdp_summed(stacked)
    first = channels + small.shape[0]
    low, high = tile_summed(chunk[:first], chunk[first:])
    w_in_grad = low[:channels]
    kernel_grad = low[channels : channels + kernel_term.shape[0]]
    gain_grad = low[channels + kernel_term.shape[0]]
    w_out_grad = high
    return (mixed, field_grad, kernel_grad, gain_grad, w_in_grad, w_out_grad)


def solution(mesh):
    return jax.shard_map(
        body,
        mesh=mesh,
        in_specs=(
            P("fsdp", None, "tile", None),
            P("tile", None),
            P(),
            P(),
            P(None, "fsdp"),
            P("fsdp", None),
            P("fsdp", None, "tile", None),
        ),
        out_specs=(
            P("fsdp", None, "tile", None),
            P("fsdp", None, "tile", None),
            P(),
            P(),
            P(None, "fsdp"),
            P("fsdp", None),
        ),
        check_vma=False,
    )
```

```python
import math

import jax
import jax.numpy as jnp
from jax import lax
from jax.sharding import PartitionSpec as P

eps = 1e-06
inv_root2 = 0.7071067811865476
inv_root_tau = 0.3989422804014327


def extended(cells, sides, width):
    for axis, dim in sides:
        count = lax.axis_size(axis)
        head = lax.slice_in_dim(cells, 0, width, axis=dim)
        tail = lax.slice_in_dim(cells, cells.shape[dim] - width, cells.shape[dim], axis=dim)
        cells = jnp.concatenate(
            [
                lax.ppermute(tail, axis, [(i, (i + 1) % count) for i in range(count)]),
                cells,
                lax.ppermute(head, axis, [((i + 1) % count, i) for i in range(count)]),
            ],
            axis=dim,
        )
    return cells


def exchange(value, axis, bit):
    count = lax.axis_size(axis)
    return lax.ppermute(value, axis, [(i, i ^ (1 << bit)) for i in range(count)])


def fsdp_summed(stacked):
    me = lax.axis_index("fsdp")
    for bit in (0, 1):
        half = stacked.shape[0] // 2
        side = (me >> bit) & 1
        keep = lax.dynamic_slice_in_dim(stacked, side * half, half, 0).astype(jnp.bfloat16)
        send = lax.dynamic_slice_in_dim(stacked, (1 - side) * half, half, 0).astype(jnp.bfloat16)
        got = exchange(send, "fsdp", bit)
        stacked = keep.astype(jnp.float32) + got.astype(jnp.float32)
    return stacked


def tile_summed(chunk):
    assert lax.axis_size("tile") == 64
    me = lax.axis_index("tile")
    groups = ((0, 1), (2, 3), (4, 5))

    def masks(group):
        mine = ((me >> group[0]) & 1) * 2 + ((me >> group[1]) & 1)
        return mine, [(d, ((d >> 1) << group[0]) | ((d & 1) << group[1])) for d in (1, 2, 3)]

    for group in groups:
        mine, partners = masks(group)
        size = chunk.shape[0] // 4
        total = lax.dynamic_slice_in_dim(chunk, mine * size, size, 0)
        for d, mask in partners:
            send = lax.dynamic_slice_in_dim(chunk, (mine ^ d) * size, size, 0)
            total = total + swapped(send.astype(jnp.bfloat16), "tile", mask).astype(jnp.float32)
        chunk = total
    chunk = chunk.astype(jnp.bfloat16)
    for group in reversed(groups):
        mine, partners = masks(group)
        size = chunk.shape[0]
        whole = jnp.zeros((4 * size,) + chunk.shape[1:], chunk.dtype)
        whole = lax.dynamic_update_slice_in_dim(whole, chunk, mine * size, 0)
        for d, mask in partners:
            got = swapped(chunk, "tile", mask)
            whole = lax.dynamic_update_slice_in_dim(whole, got, (mine ^ d) * size, 0)
        chunk = whole
    return chunk.astype(jnp.float32)


def swapped(value, axis, mask):
    count = lax.axis_size(axis)
    return lax.ppermute(value, axis, [(i, i ^ mask) for i in range(count)])


def gathered_rows(shard):
    me = lax.axis_index("fsdp")
    for bit in (0, 1):
        side = (me >> bit) & 1
        got = exchange(shard, "fsdp", bit)
        shard = jnp.concatenate(
            [jnp.where(side == 0, shard, got), jnp.where(side == 0, got, shard)], axis=0
        )
    return shard


def gelu(value):
    return value * 0.5 * (1.0 + lax.erf(value * inv_root2))


def gelu_slope(value):
    return 0.5 * (1.0 + lax.erf(value * inv_root2)) + value * inv_root_tau * jnp.exp(
        -0.5 * value * value
    )


def shift_rows(strip, offset):
    height = strip.shape[1]
    wider = jnp.pad(strip, ((0, 0), (height, height), (0, 0), (0, 0)))
    return lax.dynamic_slice_in_dim(wider, height + offset, height, 1)


def depthwise(padded, kernel):
    height = padded.shape[1] - 6
    width = padded.shape[2] - 6
    total = jnp.zeros((padded.shape[0], height, width, padded.shape[3]), jnp.float32)
    for row in range(7):
        for col in range(7):
            total = (
                total + padded[:, row : row + height, col : col + width, :] * kernel[7 * row + col]
            )
    return total


def body(fields, seam_shift, kernel, gain, w_in, w_out, cotangent):
    height = fields.shape[1]
    width = fields.shape[2]
    channels = fields.shape[3]
    count = fields.shape[0] * height * width
    cells = count * lax.axis_size("tile") * lax.axis_size("fsdp")
    factor = 1.0 / math.sqrt(cells)
    west_shift = seam_shift[0, 0]
    east_shift = seam_shift[0, 1]
    row_pad = ((0, 0), (3, 3), (0, 0), (0, 0))
    widened = extended(fields, (("tile", 2),), 3)
    west = shift_rows(widened[:, :, :3], west_shift)
    east = shift_rows(widened[:, :, width + 3 :], east_shift)
    padded = jnp.pad(jnp.concatenate([west, fields, east], axis=2), row_pad)
    mixed_in = depthwise(padded, kernel)
    rows = mixed_in.reshape(count, channels)
    mean = jnp.mean(rows, axis=-1, keepdims=True)
    centered = rows - mean
    rstd = lax.rsqrt(jnp.mean(centered * centered, axis=-1, keepdims=True) + eps)
    normed = centered * rstd
    scaled = (normed * gain).astype(jnp.bfloat16)
    back = cotangent.reshape(count, channels)
    contract_last = (((1,), (1,)), ((), ()))
    full_in, full_out = (
        lax.all_gather(w_in, "fsdp", axis=1, tiled=True),
        gathered_rows(w_out),
    )
    pre = jnp.dot(scaled, full_in, preferred_element_type=jnp.float32)
    hidden = gelu(pre).astype(jnp.bfloat16)
    branch = jnp.dot(hidden, full_out, preferred_element_type=jnp.float32)
    d_hidden = lax.dot_general(back, full_out, contract_last, preferred_element_type=jnp.float32)
    residual = fields.reshape(count, channels).astype(jnp.float32)
    mixed = (residual + branch).astype(jnp.bfloat16).reshape(fields.shape)
    d_pre = (d_hidden * gelu_slope(pre)).astype(jnp.bfloat16)
    d_scaled = lax.dot_general(d_pre, full_in, contract_last, preferred_element_type=jnp.float32)
    term_gain = jnp.sum(d_scaled * normed, axis=0) * factor
    d_normed = d_scaled * gain
    d_rows = (
        d_normed
        - jnp.mean(d_normed, axis=-1, keepdims=True)
        - normed * jnp.mean(d_normed * normed, axis=-1, keepdims=True)
    ) * rstd
    d_mixed = d_rows.reshape(mixed_in.shape)
    unused, pullback = jax.vjp(depthwise, padded.astype(jnp.float32), kernel)
    d_padded, kernel_term = pullback(d_mixed)
    kernel_term = kernel_term * factor
    d_core = d_padded[:, 3 : height + 3]
    d_west = shift_rows(d_core[:, :, :3], -west_shift)
    d_east = shift_rows(d_core[:, :, width + 3 :], -east_shift)
    returned = extended(
        jnp.concatenate([d_west, d_east], axis=2).astype(jnp.bfloat16), (("tile", 2),), 3
    ).astype(jnp.float32)
    own = cotangent.astype(jnp.float32) + d_core[:, :, 3 : width + 3]
    field_grad = jnp.concatenate(
        [
            own[:, :, :3] + returned[:, :, :3],
            own[:, :, 3 : width - 3],
            own[:, :, width - 3 :] + returned[:, :, 9:],
        ],
        axis=2,
    ).astype(jnp.bfloat16)
    parts = lax.axis_size("fsdp")
    assert parts == 4
    share = full_in.shape[1] // parts
    d_pre4 = d_pre.reshape(count, 2, 2, share)
    hidden4 = hidden.reshape(count, 2, 2, share)
    term_in4 = jnp.einsum("ck,cabh->bakh", scaled, d_pre4, preferred_element_type=jnp.float32)
    term_out4 = jnp.einsum("cabh,cj->bahj", hidden4, back, preferred_element_type=jnp.float32)
    spare = -(kernel_term.shape[0] + 1) % 64
    small = jnp.concatenate(
        [kernel_term, term_gain[None], jnp.zeros((spare, channels), jnp.float32)], axis=0
    )
    small4 = jnp.broadcast_to(small, (2, 2) + small.shape)
    stacked = jnp.concatenate(
        [
            (term_in4 * factor).astype(jnp.bfloat16),
            small4.astype(jnp.bfloat16),
            (term_out4 * factor).astype(jnp.bfloat16),
        ],
        axis=2,
    ).reshape(-1, channels)
    chunk = fsdp_summed(stacked)
    first = channels + small.shape[0]
    total = tile_summed(chunk)
    low, high = total[:first], total[first:]
    w_in_grad = low[:channels]
    kernel_grad = low[channels : channels + kernel_term.shape[0]]
    gain_grad = low[channels + kernel_term.shape[0]]
    w_out_grad = high
    return (mixed, field_grad, kernel_grad, gain_grad, w_in_grad, w_out_grad)


def solution(mesh):
    return jax.shard_map(
        body,
        mesh=mesh,
        in_specs=(
            P("fsdp", None, "tile", None),
            P("tile", None),
            P(),
            P(),
            P(None, "fsdp"),
            P("fsdp", None),
            P("fsdp", None, "tile", None),
        ),
        out_specs=(
            P("fsdp", None, "tile", None),
            P("fsdp", None, "tile", None),
            P(),
            P(),
            P(None, "fsdp"),
            P("fsdp", None),
        ),
        check_vma=False,
    )
```

```python
import math

import jax
import jax.numpy as jnp
from jax import lax
from jax.sharding import PartitionSpec as P

eps = 1e-06
inv_root2 = 0.7071067811865476
inv_root_tau = 0.3989422804014327


def extended(cells, sides, width):
    for axis, dim in sides:
        count = lax.axis_size(axis)
        head = lax.slice_in_dim(cells, 0, width, axis=dim)
        tail = lax.slice_in_dim(cells, cells.shape[dim] - width, cells.shape[dim], axis=dim)
        cells = jnp.concatenate(
            [
                lax.ppermute(tail, axis, [(i, (i + 1) % count) for i in range(count)]),
                cells,
                lax.ppermute(head, axis, [((i + 1) % count, i) for i in range(count)]),
            ],
            axis=dim,
        )
    return cells


def exchange(value, axis, bit):
    count = lax.axis_size(axis)
    return lax.ppermute(value, axis, [(i, i ^ (1 << bit)) for i in range(count)])


def fsdp_summed(stacked):
    me = lax.axis_index("fsdp")
    for bit in (0, 1):
        half = stacked.shape[0] // 2
        side = (me >> bit) & 1
        keep = lax.dynamic_slice_in_dim(stacked, side * half, half, 0).astype(jnp.bfloat16)
        send = lax.dynamic_slice_in_dim(stacked, (1 - side) * half, half, 0).astype(jnp.bfloat16)
        got = exchange(send, "fsdp", bit)
        stacked = keep.astype(jnp.float32) + got.astype(jnp.float32)
    return stacked


def tile_summed(chunk):
    assert lax.axis_size("tile") == 64
    me = lax.axis_index("tile")
    groups = ((0, 1), (2, 3), (4, 5))

    def masks(group):
        mine = ((me >> group[0]) & 1) * 2 + ((me >> group[1]) & 1)
        return mine, [(d, ((d >> 1) << group[0]) | ((d & 1) << group[1])) for d in (1, 2, 3)]

    for group in groups:
        mine, partners = masks(group)
        size = chunk.shape[0] // 4
        total = lax.dynamic_slice_in_dim(chunk, mine * size, size, 0)
        for d, mask in partners:
            send = lax.dynamic_slice_in_dim(chunk, (mine ^ d) * size, size, 0)
            total = total + swapped(send.astype(jnp.bfloat16), "tile", mask).astype(jnp.float32)
        chunk = total
    chunk = chunk.astype(jnp.bfloat16)
    for group in reversed(groups):
        mine, partners = masks(group)
        size = chunk.shape[0]
        whole = jnp.zeros((4 * size,) + chunk.shape[1:], chunk.dtype)
        whole = lax.dynamic_update_slice_in_dim(whole, chunk, mine * size, 0)
        for d, mask in partners:
            got = swapped(chunk, "tile", mask)
            whole = lax.dynamic_update_slice_in_dim(whole, got, (mine ^ d) * size, 0)
        chunk = whole
    return chunk.astype(jnp.float32)


def swapped(value, axis, mask):
    count = lax.axis_size(axis)
    return lax.ppermute(value, axis, [(i, i ^ mask) for i in range(count)])


def gathered(shard):
    me = lax.axis_index("fsdp")
    high, low = (me >> 1) & 1, me & 1
    got = exchange(shard, "fsdp", 1)
    pair = jnp.stack([jnp.where(high == 0, shard, got), jnp.where(high == 0, got, shard)])
    other = exchange(pair, "fsdp", 0)
    first, second = jnp.where(low == 0, pair, other), jnp.where(low == 0, other, pair)
    return jnp.stack([first, second], axis=1).reshape((4,) + shard.shape)


def gelu(value):
    return value * 0.5 * (1.0 + lax.erf(value * inv_root2))


def gelu_slope(value):
    return 0.5 * (1.0 + lax.erf(value * inv_root2)) + value * inv_root_tau * jnp.exp(
        -0.5 * value * value
    )


def shift_rows(strip, offset):
    height = strip.shape[1]
    wider = jnp.pad(strip, ((0, 0), (height, height), (0, 0), (0, 0)))
    return lax.dynamic_slice_in_dim(wider, height + offset, height, 1)


def depthwise(padded, kernel):
    height = padded.shape[1] - 6
    width = padded.shape[2] - 6
    total = jnp.zeros((padded.shape[0], height, width, padded.shape[3]), jnp.float32)
    for row in range(7):
        for col in range(7):
            total = (
                total + padded[:, row : row + height, col : col + width, :] * kernel[7 * row + col]
            )
    return total


def body(fields, seam_shift, kernel, gain, w_in, w_out, cotangent):
    height = fields.shape[1]
    width = fields.shape[2]
    channels = fields.shape[3]
    count = fields.shape[0] * height * width
    cells = count * lax.axis_size("tile") * lax.axis_size("fsdp")
    factor = 1.0 / math.sqrt(cells)
    west_shift = seam_shift[0, 0]
    east_shift = seam_shift[0, 1]
    row_pad = ((0, 0), (3, 3), (0, 0), (0, 0))
    widened = extended(fields, (("tile", 2),), 3)
    west = shift_rows(widened[:, :, :3], west_shift)
    east = shift_rows(widened[:, :, width + 3 :], east_shift)
    padded = jnp.pad(jnp.concatenate([west, fields, east], axis=2), row_pad)
    mixed_in = depthwise(padded, kernel)
    rows = mixed_in.reshape(count, channels)
    mean = jnp.mean(rows, axis=-1, keepdims=True)
    centered = rows - mean
    rstd = lax.rsqrt(jnp.mean(centered * centered, axis=-1, keepdims=True) + eps)
    normed = centered * rstd
    scaled = (normed * gain).astype(jnp.bfloat16)
    back = cotangent.reshape(count, channels)
    contract_last = (((1,), (1,)), ((), ()))
    both = gathered(jnp.stack([w_in, w_out]))
    full_in = jnp.moveaxis(both[:, 0], 0, 1).reshape(w_in.shape[0], -1)
    full_out = both[:, 1].reshape(-1, w_out.shape[1])
    pre = jnp.dot(scaled, full_in, preferred_element_type=jnp.float32)
    hidden = gelu(pre).astype(jnp.bfloat16)
    branch = jnp.dot(hidden, full_out, preferred_element_type=jnp.float32)
    d_hidden = lax.dot_general(back, full_out, contract_last, preferred_element_type=jnp.float32)
    residual = fields.reshape(count, channels).astype(jnp.float32)
    mixed = (residual + branch).astype(jnp.bfloat16).reshape(fields.shape)
    d_pre = (d_hidden * gelu_slope(pre)).astype(jnp.bfloat16)
    d_scaled = lax.dot_general(d_pre, full_in, contract_last, preferred_element_type=jnp.float32)
    term_gain = jnp.sum(d_scaled * normed, axis=0) * factor
    d_normed = d_scaled * gain
    d_rows = (
        d_normed
        - jnp.mean(d_normed, axis=-1, keepdims=True)
        - normed * jnp.mean(d_normed * normed, axis=-1, keepdims=True)
    ) * rstd
    d_mixed = d_rows.reshape(mixed_in.shape)
    unused, pullback = jax.vjp(depthwise, padded.astype(jnp.float32), kernel)
    d_padded, kernel_term = pullback(d_mixed)
    kernel_term = kernel_term * factor
    d_core = d_padded[:, 3 : height + 3]
    d_west = shift_rows(d_core[:, :, :3], -west_shift)
    d_east = shift_rows(d_core[:, :, width + 3 :], -east_shift)
    returned = extended(
        jnp.concatenate([d_west, d_east], axis=2).astype(jnp.bfloat16), (("tile", 2),), 3
    ).astype(jnp.float32)
    own = cotangent.astype(jnp.float32) + d_core[:, :, 3 : width + 3]
    field_grad = jnp.concatenate(
        [
            own[:, :, :3] + returned[:, :, :3],
            own[:, :, 3 : width - 3],
            own[:, :, width - 3 :] + returned[:, :, 9:],
        ],
        axis=2,
    ).astype(jnp.bfloat16)
    parts = lax.axis_size("fsdp")
    assert parts == 4
    share = full_in.shape[1] // parts
    d_pre4 = d_pre.reshape(count, 2, 2, share)
    hidden4 = hidden.reshape(count, 2, 2, share)
    term_in4 = jnp.einsum("ck,cabh->bakh", scaled, d_pre4, preferred_element_type=jnp.float32)
    term_out4 = jnp.einsum("cabh,cj->bahj", hidden4, back, preferred_element_type=jnp.float32)
    spare = -(kernel_term.shape[0] + 1) % 64
    small = jnp.concatenate(
        [kernel_term, term_gain[None], jnp.zeros((spare, channels), jnp.float32)], axis=0
    )
    small4 = jnp.broadcast_to(small, (2, 2) + small.shape)
    stacked = jnp.concatenate(
        [
            (term_in4 * factor).astype(jnp.bfloat16),
            small4.astype(jnp.bfloat16),
            (term_out4 * factor).astype(jnp.bfloat16),
        ],
        axis=2,
    ).reshape(-1, channels)
    chunk = fsdp_summed(stacked)
    first = channels + small.shape[0]
    total = tile_summed(chunk)
    low, high = total[:first], total[first:]
    w_in_grad = low[:channels]
    kernel_grad = low[channels : channels + kernel_term.shape[0]]
    gain_grad = low[channels + kernel_term.shape[0]]
    w_out_grad = high
    return (mixed, field_grad, kernel_grad, gain_grad, w_in_grad, w_out_grad)


def solution(mesh):
    return jax.shard_map(
        body,
        mesh=mesh,
        in_specs=(
            P("fsdp", None, "tile", None),
            P("tile", None),
            P(),
            P(),
            P(None, "fsdp"),
            P("fsdp", None),
            P("fsdp", None, "tile", None),
        ),
        out_specs=(
            P("fsdp", None, "tile", None),
            P("fsdp", None, "tile", None),
            P(),
            P(),
            P(None, "fsdp"),
            P("fsdp", None),
        ),
        check_vma=False,
    )
```

```python
import math

import jax
import jax.numpy as jnp
from jax import lax
from jax.sharding import PartitionSpec as P

eps = 1e-06
inv_root2 = 0.7071067811865476
inv_root_tau = 0.3989422804014327


def extended(cells, sides, width):
    for axis, dim in sides:
        count = lax.axis_size(axis)
        head = lax.slice_in_dim(cells, 0, width, axis=dim)
        tail = lax.slice_in_dim(cells, cells.shape[dim] - width, cells.shape[dim], axis=dim)
        cells = jnp.concatenate(
            [
                lax.ppermute(tail, axis, [(i, (i + 1) % count) for i in range(count)]),
                cells,
                lax.ppermute(head, axis, [((i + 1) % count, i) for i in range(count)]),
            ],
            axis=dim,
        )
    return cells


def exchange(value, axis, bit):
    count = lax.axis_size(axis)
    return lax.ppermute(value, axis, [(i, i ^ (1 << bit)) for i in range(count)])


def fsdp_summed(stacked):
    me = lax.axis_index("fsdp")
    for bit in (0, 1):
        half = stacked.shape[0] // 2
        side = (me >> bit) & 1
        keep = lax.dynamic_slice_in_dim(stacked, side * half, half, 0).astype(jnp.bfloat16)
        send = lax.dynamic_slice_in_dim(stacked, (1 - side) * half, half, 0).astype(jnp.bfloat16)
        got = exchange(send, "fsdp", bit)
        stacked = keep.astype(jnp.float32) + got.astype(jnp.float32)
    return stacked


def tile_summed(chunk):
    assert lax.axis_size("tile") == 64
    me = lax.axis_index("tile")
    groups = ((0, 1, 5), (2, 3, 4))

    def masks(group):
        k = len(group)
        mine = sum(((me >> bit) & 1) << (k - 1 - j) for j, bit in enumerate(group))
        partners = []
        for d in range(1, 1 << k):
            mask = sum(((d >> (k - 1 - j)) & 1) << bit for j, bit in enumerate(group))
            partners.append((d, mask))
        return mine, partners

    for group in groups:
        mine, partners = masks(group)
        size = chunk.shape[0] >> len(group)
        total = lax.dynamic_slice_in_dim(chunk, mine * size, size, 0)
        for d, mask in partners:
            send = lax.dynamic_slice_in_dim(chunk, (mine ^ d) * size, size, 0)
            total = total + swapped(send.astype(jnp.bfloat16), "tile", mask).astype(jnp.float32)
        chunk = total
    chunk = chunk.astype(jnp.bfloat16)
    for group in reversed(groups):
        mine, partners = masks(group)
        size = chunk.shape[0]
        whole = jnp.zeros(((size << len(group)),) + chunk.shape[1:], chunk.dtype)
        whole = lax.dynamic_update_slice_in_dim(whole, chunk, mine * size, 0)
        for d, mask in partners:
            got = swapped(chunk, "tile", mask)
            whole = lax.dynamic_update_slice_in_dim(whole, got, (mine ^ d) * size, 0)
        chunk = whole
    return chunk.astype(jnp.float32)


def swapped(value, axis, mask):
    count = lax.axis_size(axis)
    return lax.ppermute(value, axis, [(i, i ^ mask) for i in range(count)])


def gathered(shard):
    me = lax.axis_index("fsdp")
    high, low = (me >> 1) & 1, me & 1
    got = exchange(shard, "fsdp", 1)
    pair = jnp.stack([jnp.where(high == 0, shard, got), jnp.where(high == 0, got, shard)])
    other = exchange(pair, "fsdp", 0)
    first, second = jnp.where(low == 0, pair, other), jnp.where(low == 0, other, pair)
    return jnp.stack([first, second], axis=1).reshape((4,) + shard.shape)


def gelu(value):
    return value * 0.5 * (1.0 + lax.erf(value * inv_root2))


def gelu_slope(value):
    return 0.5 * (1.0 + lax.erf(value * inv_root2)) + value * inv_root_tau * jnp.exp(
        -0.5 * value * value
    )


def shift_rows(strip, offset):
    height = strip.shape[1]
    wider = jnp.pad(strip, ((0, 0), (height, height), (0, 0), (0, 0)))
    return lax.dynamic_slice_in_dim(wider, height + offset, height, 1)


def depthwise(padded, kernel):
    height = padded.shape[1] - 6
    width = padded.shape[2] - 6
    total = jnp.zeros((padded.shape[0], height, width, padded.shape[3]), jnp.float32)
    for row in range(7):
        for col in range(7):
            total = (
                total + padded[:, row : row + height, col : col + width, :] * kernel[7 * row + col]
            )
    return total


def body(fields, seam_shift, kernel, gain, w_in, w_out, cotangent):
    height = fields.shape[1]
    width = fields.shape[2]
    channels = fields.shape[3]
    count = fields.shape[0] * height * width
    cells = count * lax.axis_size("tile") * lax.axis_size("fsdp")
    factor = 1.0 / math.sqrt(cells)
    west_shift = seam_shift[0, 0]
    east_shift = seam_shift[0, 1]
    row_pad = ((0, 0), (3, 3), (0, 0), (0, 0))
    widened = extended(fields, (("tile", 2),), 3)
    west = shift_rows(widened[:, :, :3], west_shift)
    east = shift_rows(widened[:, :, width + 3 :], east_shift)
    padded = jnp.pad(jnp.concatenate([west, fields, east], axis=2), row_pad)
    mixed_in = depthwise(padded, kernel)
    rows = mixed_in.reshape(count, channels)
    mean = jnp.mean(rows, axis=-1, keepdims=True)
    centered = rows - mean
    rstd = lax.rsqrt(jnp.mean(centered * centered, axis=-1, keepdims=True) + eps)
    normed = centered * rstd
    scaled = (normed * gain).astype(jnp.bfloat16)
    back = cotangent.reshape(count, channels)
    contract_last = (((1,), (1,)), ((), ()))
    both = gathered(jnp.stack([w_in, w_out]))
    full_in = jnp.moveaxis(both[:, 0], 0, 1).reshape(w_in.shape[0], -1)
    full_out = both[:, 1].reshape(-1, w_out.shape[1])
    pre = jnp.dot(scaled, full_in, preferred_element_type=jnp.float32)
    hidden = gelu(pre).astype(jnp.bfloat16)
    branch = jnp.dot(hidden, full_out, preferred_element_type=jnp.float32)
    d_hidden = lax.dot_general(back, full_out, contract_last, preferred_element_type=jnp.float32)
    residual = fields.reshape(count, channels).astype(jnp.float32)
    mixed = (residual + branch).astype(jnp.bfloat16).reshape(fields.shape)
    d_pre = (d_hidden * gelu_slope(pre)).astype(jnp.bfloat16)
    d_scaled = lax.dot_general(d_pre, full_in, contract_last, preferred_element_type=jnp.float32)
    term_gain = jnp.sum(d_scaled * normed, axis=0) * factor
    d_normed = d_scaled * gain
    d_rows = (
        d_normed
        - jnp.mean(d_normed, axis=-1, keepdims=True)
        - normed * jnp.mean(d_normed * normed, axis=-1, keepdims=True)
    ) * rstd
    d_mixed = d_rows.reshape(mixed_in.shape)
    unused, pullback = jax.vjp(depthwise, padded.astype(jnp.float32), kernel)
    d_padded, kernel_term = pullback(d_mixed)
    kernel_term = kernel_term * factor
    d_core = d_padded[:, 3 : height + 3]
    d_west = shift_rows(d_core[:, :, :3], -west_shift)
    d_east = shift_rows(d_core[:, :, width + 3 :], -east_shift)
    returned = extended(
        jnp.concatenate([d_west, d_east], axis=2).astype(jnp.bfloat16), (("tile", 2),), 3
    ).astype(jnp.float32)
    own = cotangent.astype(jnp.float32) + d_core[:, :, 3 : width + 3]
    field_grad = jnp.concatenate(
        [
            own[:, :, :3] + returned[:, :, :3],
            own[:, :, 3 : width - 3],
            own[:, :, width - 3 :] + returned[:, :, 9:],
        ],
        axis=2,
    ).astype(jnp.bfloat16)
    parts = lax.axis_size("fsdp")
    assert parts == 4
    share = full_in.shape[1] // parts
    d_pre4 = d_pre.reshape(count, 2, 2, share)
    hidden4 = hidden.reshape(count, 2, 2, share)
    term_in4 = jnp.einsum("ck,cabh->bakh", scaled, d_pre4, preferred_element_type=jnp.float32)
    term_out4 = jnp.einsum("cabh,cj->bahj", hidden4, back, preferred_element_type=jnp.float32)
    spare = -(kernel_term.shape[0] + 1) % 64
    small = jnp.concatenate(
        [kernel_term, term_gain[None], jnp.zeros((spare, channels), jnp.float32)], axis=0
    )
    small4 = jnp.broadcast_to(small, (2, 2) + small.shape)
    stacked = jnp.concatenate(
        [
            (term_in4 * factor).astype(jnp.bfloat16),
            small4.astype(jnp.bfloat16),
            (term_out4 * factor).astype(jnp.bfloat16),
        ],
        axis=2,
    ).reshape(-1, channels)
    chunk = fsdp_summed(stacked)
    first = channels + small.shape[0]
    total = tile_summed(chunk)
    low, high = total[:first], total[first:]
    w_in_grad = low[:channels]
    kernel_grad = low[channels : channels + kernel_term.shape[0]]
    gain_grad = low[channels + kernel_term.shape[0]]
    w_out_grad = high
    return (mixed, field_grad, kernel_grad, gain_grad, w_in_grad, w_out_grad)


def solution(mesh):
    return jax.shard_map(
        body,
        mesh=mesh,
        in_specs=(
            P("fsdp", None, "tile", None),
            P("tile", None),
            P(),
            P(),
            P(None, "fsdp"),
            P("fsdp", None),
            P("fsdp", None, "tile", None),
        ),
        out_specs=(
            P("fsdp", None, "tile", None),
            P("fsdp", None, "tile", None),
            P(),
            P(),
            P(None, "fsdp"),
            P("fsdp", None),
        ),
        check_vma=False,
    )
```

```python
import math

import jax
import jax.numpy as jnp
from jax import lax
from jax.sharding import PartitionSpec as P

eps = 1e-06
inv_root2 = 0.7071067811865476
inv_root_tau = 0.3989422804014327


def extended(cells, sides, width):
    for axis, dim in sides:
        count = lax.axis_size(axis)
        head = lax.slice_in_dim(cells, 0, width, axis=dim)
        tail = lax.slice_in_dim(cells, cells.shape[dim] - width, cells.shape[dim], axis=dim)
        cells = jnp.concatenate(
            [
                lax.ppermute(tail, axis, [(i, (i + 1) % count) for i in range(count)]),
                cells,
                lax.ppermute(head, axis, [((i + 1) % count, i) for i in range(count)]),
            ],
            axis=dim,
        )
    return cells


def exchange(value, axis, bit):
    count = lax.axis_size(axis)
    return lax.ppermute(value, axis, [(i, i ^ (1 << bit)) for i in range(count)])


def fsdp_summed(stacked):
    me = lax.axis_index("fsdp")
    for bit in (0, 1):
        half = stacked.shape[0] // 2
        side = (me >> bit) & 1
        keep = lax.dynamic_slice_in_dim(stacked, side * half, half, 0).astype(jnp.bfloat16)
        send = lax.dynamic_slice_in_dim(stacked, (1 - side) * half, half, 0).astype(jnp.bfloat16)
        got = exchange(send, "fsdp", bit)
        stacked = keep.astype(jnp.float32) + got.astype(jnp.float32)
    return stacked


def tile_summed(chunk):
    assert lax.axis_size("tile") == 64
    me = lax.axis_index("tile")
    groups = ((0, 1), (2, 3), (4, 5))

    def masks(group):
        mine = ((me >> group[0]) & 1) * 2 + ((me >> group[1]) & 1)
        return mine, [(d, ((d >> 1) << group[0]) | ((d & 1) << group[1])) for d in (1, 2, 3)]

    for group in groups:
        mine, partners = masks(group)
        size = chunk.shape[0] // 4
        total = lax.dynamic_slice_in_dim(chunk, mine * size, size, 0)
        for d, mask in partners:
            send = lax.dynamic_slice_in_dim(chunk, (mine ^ d) * size, size, 0)
            total = total + swapped(send.astype(jnp.bfloat16), "tile", mask).astype(jnp.float32)
        chunk = total
    chunk = chunk.astype(jnp.bfloat16)
    for group in reversed(groups):
        mine, partners = masks(group)
        size = chunk.shape[0]
        whole = jnp.zeros((4 * size,) + chunk.shape[1:], chunk.dtype)
        whole = lax.dynamic_update_slice_in_dim(whole, chunk, mine * size, 0)
        for d, mask in partners:
            got = swapped(chunk, "tile", mask)
            whole = lax.dynamic_update_slice_in_dim(whole, got, (mine ^ d) * size, 0)
        chunk = whole
    return chunk.astype(jnp.float32)


def swapped(value, axis, mask):
    count = lax.axis_size(axis)
    return lax.ppermute(value, axis, [(i, i ^ mask) for i in range(count)])


def gathered(shard):
    me = lax.axis_index("fsdp")
    high, low = (me >> 1) & 1, me & 1
    got = exchange(shard, "fsdp", 1)
    pair = jnp.stack([jnp.where(high == 0, shard, got), jnp.where(high == 0, got, shard)])
    other = exchange(pair, "fsdp", 0)
    first, second = jnp.where(low == 0, pair, other), jnp.where(low == 0, other, pair)
    return jnp.stack([first, second], axis=1).reshape((4,) + shard.shape)


def gelu(value):
    return value * 0.5 * (1.0 + lax.erf(value * inv_root2))


def gelu_slope(value):
    return 0.5 * (1.0 + lax.erf(value * inv_root2)) + value * inv_root_tau * jnp.exp(
        -0.5 * value * value
    )


def shift_rows(strip, offset):
    height = strip.shape[1]
    wider = jnp.pad(strip, ((0, 0), (height, height), (0, 0), (0, 0)))
    return lax.dynamic_slice_in_dim(wider, height + offset, height, 1)


def depthwise(padded, kernel):
    height = padded.shape[1] - 6
    width = padded.shape[2] - 6
    total = jnp.zeros((padded.shape[0], height, width, padded.shape[3]), jnp.float32)
    for row in range(7):
        for col in range(7):
            total = (
                total + padded[:, row : row + height, col : col + width, :] * kernel[7 * row + col]
            )
    return total


def body(fields, seam_shift, kernel, gain, w_in, w_out, cotangent):
    height = fields.shape[1]
    width = fields.shape[2]
    channels = fields.shape[3]
    count = fields.shape[0] * height * width
    cells = count * lax.axis_size("tile") * lax.axis_size("fsdp")
    factor = 1.0 / math.sqrt(cells)
    west_shift = seam_shift[0, 0]
    east_shift = seam_shift[0, 1]
    row_pad = ((0, 0), (3, 3), (0, 0), (0, 0))
    widened = extended(fields, (("tile", 2),), 3)
    west = shift_rows(widened[:, :, :3], west_shift)
    east = shift_rows(widened[:, :, width + 3 :], east_shift)
    padded = jnp.pad(jnp.concatenate([west, fields, east], axis=2), row_pad)
    mixed_in = depthwise(padded, kernel)
    rows = mixed_in.reshape(count, channels)
    mean = jnp.mean(rows, axis=-1, keepdims=True)
    centered = rows - mean
    rstd = lax.rsqrt(jnp.mean(centered * centered, axis=-1, keepdims=True) + eps)
    normed = centered * rstd
    scaled = (normed * gain).astype(jnp.bfloat16)
    back = cotangent.reshape(count, channels)
    contract_last = (((1,), (1,)), ((), ()))
    both = gathered(jnp.stack([w_in, w_out]))
    full_in = jnp.concatenate([both[f, 0] for f in range(both.shape[0])], axis=1)
    full_out = both[:, 1].reshape(-1, w_out.shape[1])
    pre = jnp.dot(scaled, full_in, preferred_element_type=jnp.float32)
    hidden = gelu(pre).astype(jnp.bfloat16)
    branch = jnp.dot(hidden, full_out, preferred_element_type=jnp.float32)
    d_hidden = lax.dot_general(back, full_out, contract_last, preferred_element_type=jnp.float32)
    residual = fields.reshape(count, channels).astype(jnp.float32)
    mixed = (residual + branch).astype(jnp.bfloat16).reshape(fields.shape)
    d_pre = (d_hidden * gelu_slope(pre)).astype(jnp.bfloat16)
    d_scaled = lax.dot_general(d_pre, full_in, contract_last, preferred_element_type=jnp.float32)
    term_gain = jnp.sum(d_scaled * normed, axis=0) * factor
    d_normed = d_scaled * gain
    d_rows = (
        d_normed
        - jnp.mean(d_normed, axis=-1, keepdims=True)
        - normed * jnp.mean(d_normed * normed, axis=-1, keepdims=True)
    ) * rstd
    d_mixed = d_rows.reshape(mixed_in.shape)
    unused, pullback = jax.vjp(depthwise, padded.astype(jnp.float32), kernel)
    d_padded, kernel_term = pullback(d_mixed)
    kernel_term = kernel_term * factor
    d_core = d_padded[:, 3 : height + 3]
    d_west = shift_rows(d_core[:, :, :3], -west_shift)
    d_east = shift_rows(d_core[:, :, width + 3 :], -east_shift)
    returned = extended(
        jnp.concatenate([d_west, d_east], axis=2).astype(jnp.bfloat16), (("tile", 2),), 3
    ).astype(jnp.float32)
    own = cotangent.astype(jnp.float32) + d_core[:, :, 3 : width + 3]
    field_grad = jnp.concatenate(
        [
            own[:, :, :3] + returned[:, :, :3],
            own[:, :, 3 : width - 3],
            own[:, :, width - 3 :] + returned[:, :, 9:],
        ],
        axis=2,
    ).astype(jnp.bfloat16)
    parts = lax.axis_size("fsdp")
    assert parts == 4
    share = full_in.shape[1] // parts
    owners = [0, 2, 1, 3]
    contract_rows = (((0,), (0,)), ((), ()))
    term_in4 = jnp.stack(
        [
            lax.dot_general(
                scaled, d_pre[:, f * share : (f + 1) * share], contract_rows,
                preferred_element_type=jnp.float32,
            )
            for f in owners
        ]
    ).reshape(2, 2, channels, share)
    term_out4 = jnp.stack(
        [
            lax.dot_general(
                hidden[:, f * share : (f + 1) * share], back, contract_rows,
                preferred_element_type=jnp.float32,
            )
            for f in owners
        ]
    ).reshape(2, 2, share, channels)
    spare = -(kernel_term.shape[0] + 1) % 64
    small = jnp.concatenate(
        [kernel_term, term_gain[None], jnp.zeros((spare, channels), jnp.float32)], axis=0
    )
    small4 = jnp.broadcast_to(small, (2, 2) + small.shape)
    stacked = jnp.concatenate(
        [
            (term_in4 * factor).astype(jnp.bfloat16),
            small4.astype(jnp.bfloat16),
            (term_out4 * factor).astype(jnp.bfloat16),
        ],
        axis=2,
    ).reshape(-1, channels)
    chunk = fsdp_summed(stacked)
    first = channels + small.shape[0]
    total = tile_summed(chunk)
    low, high = total[:first], total[first:]
    w_in_grad = low[:channels]
    kernel_grad = low[channels : channels + kernel_term.shape[0]]
    gain_grad = low[channels + kernel_term.shape[0]]
    w_out_grad = high
    return (mixed, field_grad, kernel_grad, gain_grad, w_in_grad, w_out_grad)


def solution(mesh):
    return jax.shard_map(
        body,
        mesh=mesh,
        in_specs=(
            P("fsdp", None, "tile", None),
            P("tile", None),
            P(),
            P(),
            P(None, "fsdp"),
            P("fsdp", None),
            P("fsdp", None, "tile", None),
        ),
        out_specs=(
            P("fsdp", None, "tile", None),
            P("fsdp", None, "tile", None),
            P(),
            P(),
            P(None, "fsdp"),
            P("fsdp", None),
        ),
        check_vma=False,
    )
```

```python
import math

import jax
import jax.numpy as jnp
from jax import lax
from jax.sharding import PartitionSpec as P

eps = 1e-06
inv_root2 = 0.7071067811865476
inv_root_tau = 0.3989422804014327


def extended(cells, sides, width):
    for axis, dim in sides:
        count = lax.axis_size(axis)
        head = lax.slice_in_dim(cells, 0, width, axis=dim)
        tail = lax.slice_in_dim(cells, cells.shape[dim] - width, cells.shape[dim], axis=dim)
        cells = jnp.concatenate(
            [
                lax.ppermute(tail, axis, [(i, (i + 1) % count) for i in range(count)]),
                cells,
                lax.ppermute(head, axis, [((i + 1) % count, i) for i in range(count)]),
            ],
            axis=dim,
        )
    return cells


def exchange(value, axis, bit):
    count = lax.axis_size(axis)
    return lax.ppermute(value, axis, [(i, i ^ (1 << bit)) for i in range(count)])


def fsdp_summed(stacked):
    me = lax.axis_index("fsdp")
    for bit in (0, 1):
        half = stacked.shape[0] // 2
        side = (me >> bit) & 1
        keep = lax.dynamic_slice_in_dim(stacked, side * half, half, 0).astype(jnp.bfloat16)
        send = lax.dynamic_slice_in_dim(stacked, (1 - side) * half, half, 0).astype(jnp.bfloat16)
        got = exchange(send, "fsdp", bit)
        stacked = keep.astype(jnp.float32) + got.astype(jnp.float32)
    return stacked


def tile_summed(chunk):
    assert lax.axis_size("tile") == 64
    me = lax.axis_index("tile")
    groups = ((0, 1), (2, 3), (4, 5))

    def masks(group):
        mine = ((me >> group[0]) & 1) * 2 + ((me >> group[1]) & 1)
        return mine, [(d, ((d >> 1) << group[0]) | ((d & 1) << group[1])) for d in (1, 2, 3)]

    for group in groups[:-1]:
        mine, partners = masks(group)
        size = chunk.shape[0] // 4
        total = lax.dynamic_slice_in_dim(chunk, mine * size, size, 0)
        for d, mask in partners:
            send = lax.dynamic_slice_in_dim(chunk, (mine ^ d) * size, size, 0)
            total = total + swapped(send.astype(jnp.bfloat16), "tile", mask).astype(jnp.float32)
        chunk = total
    mine, partners = masks(groups[-1])
    own = chunk.astype(jnp.bfloat16)
    blocks = jnp.stack([own] + [swapped(own, "tile", mask) for _, mask in partners])
    total = None
    for place in range(4):
        block = lax.dynamic_index_in_dim(blocks, place ^ mine, 0, keepdims=False).astype(jnp.float32)
        total = block if total is None else total + block
    chunk = total.astype(jnp.bfloat16)
    for group in reversed(groups[:-1]):
        mine, partners = masks(group)
        size = chunk.shape[0]
        whole = jnp.zeros((4 * size,) + chunk.shape[1:], chunk.dtype)
        whole = lax.dynamic_update_slice_in_dim(whole, chunk, mine * size, 0)
        for d, mask in partners:
            got = swapped(chunk, "tile", mask)
            whole = lax.dynamic_update_slice_in_dim(whole, got, (mine ^ d) * size, 0)
        chunk = whole
    return chunk.astype(jnp.float32)


def swapped(value, axis, mask):
    count = lax.axis_size(axis)
    return lax.ppermute(value, axis, [(i, i ^ mask) for i in range(count)])


def gathered(shard):
    me = lax.axis_index("fsdp")
    high, low = (me >> 1) & 1, me & 1
    got = exchange(shard, "fsdp", 1)
    pair = jnp.stack([jnp.where(high == 0, shard, got), jnp.where(high == 0, got, shard)])
    other = exchange(pair, "fsdp", 0)
    first, second = jnp.where(low == 0, pair, other), jnp.where(low == 0, other, pair)
    return jnp.stack([first, second], axis=1).reshape((4,) + shard.shape)


def gelu(value):
    return value * 0.5 * (1.0 + lax.erf(value * inv_root2))


def gelu_slope(value):
    return 0.5 * (1.0 + lax.erf(value * inv_root2)) + value * inv_root_tau * jnp.exp(
        -0.5 * value * value
    )


def shift_rows(strip, offset):
    height = strip.shape[1]
    wider = jnp.pad(strip, ((0, 0), (height, height), (0, 0), (0, 0)))
    return lax.dynamic_slice_in_dim(wider, height + offset, height, 1)


def depthwise(padded, kernel):
    height = padded.shape[1] - 6
    width = padded.shape[2] - 6
    total = jnp.zeros((padded.shape[0], height, width, padded.shape[3]), jnp.float32)
    for row in range(7):
        for col in range(7):
            total = (
                total + padded[:, row : row + height, col : col + width, :] * kernel[7 * row + col]
            )
    return total


def body(fields, seam_shift, kernel, gain, w_in, w_out, cotangent):
    height = fields.shape[1]
    width = fields.shape[2]
    channels = fields.shape[3]
    count = fields.shape[0] * height * width
    cells = count * lax.axis_size("tile") * lax.axis_size("fsdp")
    factor = 1.0 / math.sqrt(cells)
    west_shift = seam_shift[0, 0]
    east_shift = seam_shift[0, 1]
    row_pad = ((0, 0), (3, 3), (0, 0), (0, 0))
    widened = extended(fields, (("tile", 2),), 3)
    west = shift_rows(widened[:, :, :3], west_shift)
    east = shift_rows(widened[:, :, width + 3 :], east_shift)
    padded = jnp.pad(jnp.concatenate([west, fields, east], axis=2), row_pad)
    mixed_in = depthwise(padded, kernel)
    rows = mixed_in.reshape(count, channels)
    mean = jnp.mean(rows, axis=-1, keepdims=True)
    centered = rows - mean
    rstd = lax.rsqrt(jnp.mean(centered * centered, axis=-1, keepdims=True) + eps)
    normed = centered * rstd
    scaled = (normed * gain).astype(jnp.bfloat16)
    back = cotangent.reshape(count, channels)
    contract_last = (((1,), (1,)), ((), ()))
    both = gathered(jnp.stack([w_in, w_out]))
    full_in = jnp.concatenate([both[f, 0] for f in range(both.shape[0])], axis=1)
    full_out = both[:, 1].reshape(-1, w_out.shape[1])
    pre = jnp.dot(scaled, full_in, preferred_element_type=jnp.float32)
    hidden = gelu(pre).astype(jnp.bfloat16)
    branch = jnp.dot(hidden, full_out, preferred_element_type=jnp.float32)
    d_hidden = lax.dot_general(back, full_out, contract_last, preferred_element_type=jnp.float32)
    residual = fields.reshape(count, channels).astype(jnp.float32)
    mixed = (residual + branch).astype(jnp.bfloat16).reshape(fields.shape)
    d_pre = (d_hidden * gelu_slope(pre)).astype(jnp.bfloat16)
    d_scaled = lax.dot_general(d_pre, full_in, contract_last, preferred_element_type=jnp.float32)
    term_gain = jnp.sum(d_scaled * normed, axis=0) * factor
    d_normed = d_scaled * gain
    d_rows = (
        d_normed
        - jnp.mean(d_normed, axis=-1, keepdims=True)
        - normed * jnp.mean(d_normed * normed, axis=-1, keepdims=True)
    ) * rstd
    d_mixed = d_rows.reshape(mixed_in.shape)
    unused, pullback = jax.vjp(depthwise, padded.astype(jnp.float32), kernel)
    d_padded, kernel_term = pullback(d_mixed)
    kernel_term = kernel_term * factor
    d_core = d_padded[:, 3 : height + 3]
    d_west = shift_rows(d_core[:, :, :3], -west_shift)
    d_east = shift_rows(d_core[:, :, width + 3 :], -east_shift)
    returned = extended(
        jnp.concatenate([d_west, d_east], axis=2).astype(jnp.bfloat16), (("tile", 2),), 3
    ).astype(jnp.float32)
    own = cotangent.astype(jnp.float32) + d_core[:, :, 3 : width + 3]
    field_grad = jnp.concatenate(
        [
            own[:, :, :3] + returned[:, :, :3],
            own[:, :, 3 : width - 3],
            own[:, :, width - 3 :] + returned[:, :, 9:],
        ],
        axis=2,
    ).astype(jnp.bfloat16)
    parts = lax.axis_size("fsdp")
    assert parts == 4
    share = full_in.shape[1] // parts
    owners = [0, 2, 1, 3]
    contract_rows = (((0,), (0,)), ((), ()))
    term_in4 = jnp.stack(
        [
            lax.dot_general(
                scaled, d_pre[:, f * share : (f + 1) * share], contract_rows,
                preferred_element_type=jnp.float32,
            )
            for f in owners
        ]
    ).reshape(2, 2, channels, share)
    term_out4 = jnp.stack(
        [
            lax.dot_general(
                hidden[:, f * share : (f + 1) * share], back, contract_rows,
                preferred_element_type=jnp.float32,
            )
            for f in owners
        ]
    ).reshape(2, 2, share, channels)
    spare = -(kernel_term.shape[0] + 1) % 64
    small = jnp.concatenate(
        [kernel_term, term_gain[None], jnp.zeros((spare, channels), jnp.float32)], axis=0
    )
    small4 = jnp.broadcast_to(small, (2, 2) + small.shape)
    stacked = jnp.concatenate(
        [
            (term_in4 * factor).astype(jnp.bfloat16),
            small4.astype(jnp.bfloat16),
            (term_out4 * factor).astype(jnp.bfloat16),
        ],
        axis=2,
    ).reshape(-1, channels)
    chunk = fsdp_summed(stacked)
    first = channels + small.shape[0]
    total = tile_summed(chunk)
    low, high = total[:first], total[first:]
    w_in_grad = low[:channels]
    kernel_grad = low[channels : channels + kernel_term.shape[0]]
    gain_grad = low[channels + kernel_term.shape[0]]
    w_out_grad = high
    return (mixed, field_grad, kernel_grad, gain_grad, w_in_grad, w_out_grad)


def solution(mesh):
    return jax.shard_map(
        body,
        mesh=mesh,
        in_specs=(
            P("fsdp", None, "tile", None),
            P("tile", None),
            P(),
            P(),
            P(None, "fsdp"),
            P("fsdp", None),
            P("fsdp", None, "tile", None),
        ),
        out_specs=(
            P("fsdp", None, "tile", None),
            P("fsdp", None, "tile", None),
            P(),
            P(),
            P(None, "fsdp"),
            P("fsdp", None),
        ),
        check_vma=False,
    )
```

```python
import math

import jax
import jax.numpy as jnp
from jax import lax
from jax.sharding import PartitionSpec as P

eps = 1e-06
inv_root2 = 0.7071067811865476
inv_root_tau = 0.3989422804014327


def extended(cells, sides, width):
    for axis, dim in sides:
        count = lax.axis_size(axis)
        head = lax.slice_in_dim(cells, 0, width, axis=dim)
        tail = lax.slice_in_dim(cells, cells.shape[dim] - width, cells.shape[dim], axis=dim)
        cells = jnp.concatenate(
            [
                lax.ppermute(tail, axis, [(i, (i + 1) % count) for i in range(count)]),
                cells,
                lax.ppermute(head, axis, [((i + 1) % count, i) for i in range(count)]),
            ],
            axis=dim,
        )
    return cells


def exchange(value, axis, bit):
    count = lax.axis_size(axis)
    return lax.ppermute(value, axis, [(i, i ^ (1 << bit)) for i in range(count)])


def fsdp_summed(stacked):
    me = lax.axis_index("fsdp")
    for bit in (0, 1):
        half = stacked.shape[0] // 2
        side = (me >> bit) & 1
        keep = lax.dynamic_slice_in_dim(stacked, side * half, half, 0).astype(jnp.bfloat16)
        send = lax.dynamic_slice_in_dim(stacked, (1 - side) * half, half, 0).astype(jnp.bfloat16)
        got = exchange(send, "fsdp", bit)
        stacked = keep.astype(jnp.float32) + got.astype(jnp.float32)
    return stacked


def tile_summed(chunk):
    assert lax.axis_size("tile") == 64
    me = lax.axis_index("tile")
    groups = ((0, 1), (2, 3), (4, 5))

    def masks(group):
        mine = ((me >> group[0]) & 1) * 2 + ((me >> group[1]) & 1)
        return mine, [(d, ((d >> 1) << group[0]) | ((d & 1) << group[1])) for d in (1, 2, 3)]

    for group in groups[:1]:
        mine, partners = masks(group)
        size = chunk.shape[0] // 4
        total = lax.dynamic_slice_in_dim(chunk, mine * size, size, 0)
        for d, mask in partners:
            send = lax.dynamic_slice_in_dim(chunk, (mine ^ d) * size, size, 0)
            total = total + swapped(send.astype(jnp.bfloat16), "tile", mask).astype(jnp.float32)
        chunk = total
    chunk = chunk.astype(jnp.bfloat16)
    for group in groups[1:]:
        mine, partners = masks(group)
        blocks = jnp.stack([chunk] + [swapped(chunk, "tile", mask) for _, mask in partners])
        total = None
        for place in range(4):
            block = lax.dynamic_index_in_dim(blocks, place ^ mine, 0, keepdims=False)
            block = block.astype(jnp.float32)
            total = block if total is None else total + block
        chunk = total.astype(jnp.bfloat16)
    for group in reversed(groups[:1]):
        mine, partners = masks(group)
        size = chunk.shape[0]
        whole = jnp.zeros((4 * size,) + chunk.shape[1:], chunk.dtype)
        whole = lax.dynamic_update_slice_in_dim(whole, chunk, mine * size, 0)
        for d, mask in partners:
            got = swapped(chunk, "tile", mask)
            whole = lax.dynamic_update_slice_in_dim(whole, got, (mine ^ d) * size, 0)
        chunk = whole
    return chunk.astype(jnp.float32)


def swapped(value, axis, mask):
    count = lax.axis_size(axis)
    return lax.ppermute(value, axis, [(i, i ^ mask) for i in range(count)])


def gathered(shard):
    me = lax.axis_index("fsdp")
    high, low = (me >> 1) & 1, me & 1
    got = exchange(shard, "fsdp", 1)
    pair = jnp.stack([jnp.where(high == 0, shard, got), jnp.where(high == 0, got, shard)])
    other = exchange(pair, "fsdp", 0)
    first, second = jnp.where(low == 0, pair, other), jnp.where(low == 0, other, pair)
    return jnp.stack([first, second], axis=1).reshape((4,) + shard.shape)


def gelu(value):
    return value * 0.5 * (1.0 + lax.erf(value * inv_root2))


def gelu_slope(value):
    return 0.5 * (1.0 + lax.erf(value * inv_root2)) + value * inv_root_tau * jnp.exp(
        -0.5 * value * value
    )


def shift_rows(strip, offset):
    height = strip.shape[1]
    wider = jnp.pad(strip, ((0, 0), (height, height), (0, 0), (0, 0)))
    return lax.dynamic_slice_in_dim(wider, height + offset, height, 1)


def depthwise(padded, kernel):
    height = padded.shape[1] - 6
    width = padded.shape[2] - 6
    total = jnp.zeros((padded.shape[0], height, width, padded.shape[3]), jnp.float32)
    for row in range(7):
        for col in range(7):
            total = (
                total + padded[:, row : row + height, col : col + width, :] * kernel[7 * row + col]
            )
    return total


def body(fields, seam_shift, kernel, gain, w_in, w_out, cotangent):
    height = fields.shape[1]
    width = fields.shape[2]
    channels = fields.shape[3]
    count = fields.shape[0] * height * width
    cells = count * lax.axis_size("tile") * lax.axis_size("fsdp")
    factor = 1.0 / math.sqrt(cells)
    west_shift = seam_shift[0, 0]
    east_shift = seam_shift[0, 1]
    row_pad = ((0, 0), (3, 3), (0, 0), (0, 0))
    widened = extended(fields, (("tile", 2),), 3)
    west = shift_rows(widened[:, :, :3], west_shift)
    east = shift_rows(widened[:, :, width + 3 :], east_shift)
    padded = jnp.pad(jnp.concatenate([west, fields, east], axis=2), row_pad)
    mixed_in = depthwise(padded, kernel)
    rows = mixed_in.reshape(count, channels)
    mean = jnp.mean(rows, axis=-1, keepdims=True)
    centered = rows - mean
    rstd = lax.rsqrt(jnp.mean(centered * centered, axis=-1, keepdims=True) + eps)
    normed = centered * rstd
    scaled = (normed * gain).astype(jnp.bfloat16)
    back = cotangent.reshape(count, channels)
    contract_last = (((1,), (1,)), ((), ()))
    both = gathered(jnp.stack([w_in, w_out]))
    full_in = jnp.concatenate([both[f, 0] for f in range(both.shape[0])], axis=1)
    full_out = both[:, 1].reshape(-1, w_out.shape[1])
    pre = jnp.dot(scaled, full_in, preferred_element_type=jnp.float32)
    hidden = gelu(pre).astype(jnp.bfloat16)
    branch = jnp.dot(hidden, full_out, preferred_element_type=jnp.float32)
    d_hidden = lax.dot_general(back, full_out, contract_last, preferred_element_type=jnp.float32)
    residual = fields.reshape(count, channels).astype(jnp.float32)
    mixed = (residual + branch).astype(jnp.bfloat16).reshape(fields.shape)
    d_pre = (d_hidden * gelu_slope(pre)).astype(jnp.bfloat16)
    d_scaled = lax.dot_general(d_pre, full_in, contract_last, preferred_element_type=jnp.float32)
    term_gain = jnp.sum(d_scaled * normed, axis=0) * factor
    d_normed = d_scaled * gain
    d_rows = (
        d_normed
        - jnp.mean(d_normed, axis=-1, keepdims=True)
        - normed * jnp.mean(d_normed * normed, axis=-1, keepdims=True)
    ) * rstd
    d_mixed = d_rows.reshape(mixed_in.shape)
    unused, pullback = jax.vjp(depthwise, padded.astype(jnp.float32), kernel)
    d_padded, kernel_term = pullback(d_mixed)
    kernel_term = kernel_term * factor
    d_core = d_padded[:, 3 : height + 3]
    d_west = shift_rows(d_core[:, :, :3], -west_shift)
    d_east = shift_rows(d_core[:, :, width + 3 :], -east_shift)
    returned = extended(
        jnp.concatenate([d_west, d_east], axis=2).astype(jnp.bfloat16), (("tile", 2),), 3
    ).astype(jnp.float32)
    own = cotangent.astype(jnp.float32) + d_core[:, :, 3 : width + 3]
    field_grad = jnp.concatenate(
        [
            own[:, :, :3] + returned[:, :, :3],
            own[:, :, 3 : width - 3],
            own[:, :, width - 3 :] + returned[:, :, 9:],
        ],
        axis=2,
    ).astype(jnp.bfloat16)
    parts = lax.axis_size("fsdp")
    assert parts == 4
    share = full_in.shape[1] // parts
    owners = [0, 2, 1, 3]
    contract_rows = (((0,), (0,)), ((), ()))
    term_in4 = jnp.stack(
        [
            lax.dot_general(
                scaled, d_pre[:, f * share : (f + 1) * share], contract_rows,
                preferred_element_type=jnp.float32,
            )
            for f in owners
        ]
    ).reshape(2, 2, channels, share)
    term_out4 = jnp.stack(
        [
            lax.dot_general(
                hidden[:, f * share : (f + 1) * share], back, contract_rows,
                preferred_element_type=jnp.float32,
            )
            for f in owners
        ]
    ).reshape(2, 2, share, channels)
    spare = -(kernel_term.shape[0] + 1) % 64
    small = jnp.concatenate(
        [kernel_term, term_gain[None], jnp.zeros((spare, channels), jnp.float32)], axis=0
    )
    small4 = jnp.broadcast_to(small, (2, 2) + small.shape)
    stacked = jnp.concatenate(
        [
            (term_in4 * factor).astype(jnp.bfloat16),
            small4.astype(jnp.bfloat16),
            (term_out4 * factor).astype(jnp.bfloat16),
        ],
        axis=2,
    ).reshape(-1, channels)
    chunk = fsdp_summed(stacked)
    first = channels + small.shape[0]
    total = tile_summed(chunk)
    low, high = total[:first], total[first:]
    w_in_grad = low[:channels]
    kernel_grad = low[channels : channels + kernel_term.shape[0]]
    gain_grad = low[channels + kernel_term.shape[0]]
    w_out_grad = high
    return (mixed, field_grad, kernel_grad, gain_grad, w_in_grad, w_out_grad)


def solution(mesh):
    return jax.shard_map(
        body,
        mesh=mesh,
        in_specs=(
            P("fsdp", None, "tile", None),
            P("tile", None),
            P(),
            P(),
            P(None, "fsdp"),
            P("fsdp", None),
            P("fsdp", None, "tile", None),
        ),
        out_specs=(
            P("fsdp", None, "tile", None),
            P("fsdp", None, "tile", None),
            P(),
            P(),
            P(None, "fsdp"),
            P("fsdp", None),
        ),
        check_vma=False,
    )
```

```python
import math

import jax
import jax.numpy as jnp
from jax import lax
from jax.sharding import PartitionSpec as P

eps = 1e-06
inv_root2 = 0.7071067811865476
inv_root_tau = 0.3989422804014327


def extended(cells, sides, width):
    for axis, dim in sides:
        count = lax.axis_size(axis)
        head = lax.slice_in_dim(cells, 0, width, axis=dim)
        tail = lax.slice_in_dim(cells, cells.shape[dim] - width, cells.shape[dim], axis=dim)
        cells = jnp.concatenate(
            [
                lax.ppermute(tail, axis, [(i, (i + 1) % count) for i in range(count)]),
                cells,
                lax.ppermute(head, axis, [((i + 1) % count, i) for i in range(count)]),
            ],
            axis=dim,
        )
    return cells


def exchange(value, axis, bit):
    count = lax.axis_size(axis)
    return lax.ppermute(value, axis, [(i, i ^ (1 << bit)) for i in range(count)])


def fsdp_summed(stacked):
    me = lax.axis_index("fsdp")
    for bit in (0, 1):
        half = stacked.shape[0] // 2
        side = (me >> bit) & 1
        keep = lax.dynamic_slice_in_dim(stacked, side * half, half, 0).astype(jnp.bfloat16)
        send = lax.dynamic_slice_in_dim(stacked, (1 - side) * half, half, 0).astype(jnp.bfloat16)
        got = exchange(send, "fsdp", bit)
        stacked = keep.astype(jnp.float32) + got.astype(jnp.float32)
    return stacked


def tile_summed(chunk):
    assert lax.axis_size("tile") == 64
    me = lax.axis_index("tile")
    groups = ((0, 1), (2, 3), (4, 5))

    def masks(group):
        mine = ((me >> group[0]) & 1) * 2 + ((me >> group[1]) & 1)
        return mine, [(d, ((d >> 1) << group[0]) | ((d & 1) << group[1])) for d in (1, 2, 3)]

    for group in groups[:-1]:
        mine, partners = masks(group)
        size = chunk.shape[0] // 4
        total = lax.dynamic_slice_in_dim(chunk, mine * size, size, 0)
        for d, mask in partners:
            send = lax.dynamic_slice_in_dim(chunk, (mine ^ d) * size, size, 0)
            total = total + swapped(send.astype(jnp.bfloat16), "tile", mask).astype(jnp.float32)
        chunk = total
    mine, partners = masks(groups[-1])
    own = chunk.astype(jnp.bfloat16)
    blocks = jnp.stack([own] + [swapped(own, "tile", mask) for _, mask in partners])
    total = None
    for place in range(4):
        block = lax.dynamic_index_in_dim(blocks, place ^ mine, 0, keepdims=False).astype(jnp.float32)
        total = block if total is None else total + block
    chunk = total.astype(jnp.bfloat16)
    for group in reversed(groups[:-1]):
        mine, partners = masks(group)
        size = chunk.shape[0]
        whole = jnp.zeros((4 * size,) + chunk.shape[1:], chunk.dtype)
        whole = lax.dynamic_update_slice_in_dim(whole, chunk, mine * size, 0)
        for d, mask in partners:
            got = swapped(chunk, "tile", mask)
            whole = lax.dynamic_update_slice_in_dim(whole, got, (mine ^ d) * size, 0)
        chunk = whole
    return chunk.astype(jnp.float32)


def swapped(value, axis, mask):
    count = lax.axis_size(axis)
    return lax.ppermute(value, axis, [(i, i ^ mask) for i in range(count)])


def gathered(shard, anchor):
    me = lax.axis_index("fsdp")
    high, low = (me >> 1) & 1, me & 1
    got = exchange(shard, "fsdp", 1)
    pair = jnp.stack([jnp.where(high == 0, shard, got), jnp.where(high == 0, got, shard)])
    pair, anchor = lax.optimization_barrier((pair, anchor))
    other = exchange(pair, "fsdp", 0)
    first, second = jnp.where(low == 0, pair, other), jnp.where(low == 0, other, pair)
    return jnp.stack([first, second], axis=1).reshape((4,) + shard.shape), anchor


def gelu(value):
    return value * 0.5 * (1.0 + lax.erf(value * inv_root2))


def gelu_slope(value):
    return 0.5 * (1.0 + lax.erf(value * inv_root2)) + value * inv_root_tau * jnp.exp(
        -0.5 * value * value
    )


def shift_rows(strip, offset):
    height = strip.shape[1]
    wider = jnp.pad(strip, ((0, 0), (height, height), (0, 0), (0, 0)))
    return lax.dynamic_slice_in_dim(wider, height + offset, height, 1)


def depthwise(padded, kernel):
    height = padded.shape[1] - 6
    width = padded.shape[2] - 6
    total = jnp.zeros((padded.shape[0], height, width, padded.shape[3]), jnp.float32)
    for row in range(7):
        for col in range(7):
            total = (
                total + padded[:, row : row + height, col : col + width, :] * kernel[7 * row + col]
            )
    return total


def body(fields, seam_shift, kernel, gain, w_in, w_out, cotangent):
    height = fields.shape[1]
    width = fields.shape[2]
    channels = fields.shape[3]
    count = fields.shape[0] * height * width
    cells = count * lax.axis_size("tile") * lax.axis_size("fsdp")
    factor = 1.0 / math.sqrt(cells)
    west_shift = seam_shift[0, 0]
    east_shift = seam_shift[0, 1]
    row_pad = ((0, 0), (3, 3), (0, 0), (0, 0))
    widened = extended(fields, (("tile", 2),), 3)
    west = shift_rows(widened[:, :, :3], west_shift)
    east = shift_rows(widened[:, :, width + 3 :], east_shift)
    padded = jnp.pad(jnp.concatenate([west, fields, east], axis=2), row_pad)
    mixed_in = depthwise(padded, kernel)
    rows = mixed_in.reshape(count, channels)
    mean = jnp.mean(rows, axis=-1, keepdims=True)
    centered = rows - mean
    rstd = lax.rsqrt(jnp.mean(centered * centered, axis=-1, keepdims=True) + eps)
    normed = centered * rstd
    scaled = (normed * gain).astype(jnp.bfloat16)
    back = cotangent.reshape(count, channels)
    contract_last = (((1,), (1,)), ((), ()))
    both, scaled = gathered(jnp.stack([w_in, w_out]), scaled)
    full_in = jnp.concatenate([both[f, 0] for f in range(both.shape[0])], axis=1)
    full_out = both[:, 1].reshape(-1, w_out.shape[1])
    pre = jnp.dot(scaled, full_in, preferred_element_type=jnp.float32)
    hidden = gelu(pre).astype(jnp.bfloat16)
    branch = jnp.dot(hidden, full_out, preferred_element_type=jnp.float32)
    d_hidden = lax.dot_general(back, full_out, contract_last, preferred_element_type=jnp.float32)
    residual = fields.reshape(count, channels).astype(jnp.float32)
    mixed = (residual + branch).astype(jnp.bfloat16).reshape(fields.shape)
    d_pre = (d_hidden * gelu_slope(pre)).astype(jnp.bfloat16)
    d_scaled = lax.dot_general(d_pre, full_in, contract_last, preferred_element_type=jnp.float32)
    term_gain = jnp.sum(d_scaled * normed, axis=0) * factor
    d_normed = d_scaled * gain
    d_rows = (
        d_normed
        - jnp.mean(d_normed, axis=-1, keepdims=True)
        - normed * jnp.mean(d_normed * normed, axis=-1, keepdims=True)
    ) * rstd
    d_mixed = d_rows.reshape(mixed_in.shape)
    unused, pullback = jax.vjp(depthwise, padded.astype(jnp.float32), kernel)
    d_padded, kernel_term = pullback(d_mixed)
    kernel_term = kernel_term * factor
    d_core = d_padded[:, 3 : height + 3]
    d_west = shift_rows(d_core[:, :, :3], -west_shift)
    d_east = shift_rows(d_core[:, :, width + 3 :], -east_shift)
    returned = extended(
        jnp.concatenate([d_west, d_east], axis=2).astype(jnp.bfloat16), (("tile", 2),), 3
    ).astype(jnp.float32)
    own = cotangent.astype(jnp.float32) + d_core[:, :, 3 : width + 3]
    field_grad = jnp.concatenate(
        [
            own[:, :, :3] + returned[:, :, :3],
            own[:, :, 3 : width - 3],
            own[:, :, width - 3 :] + returned[:, :, 9:],
        ],
        axis=2,
    ).astype(jnp.bfloat16)
    parts = lax.axis_size("fsdp")
    assert parts == 4
    share = full_in.shape[1] // parts
    owners = [0, 2, 1, 3]
    contract_rows = (((0,), (0,)), ((), ()))
    term_in4 = jnp.stack(
        [
            lax.dot_general(
                scaled, d_pre[:, f * share : (f + 1) * share], contract_rows,
                preferred_element_type=jnp.float32,
            )
            for f in owners
        ]
    ).reshape(2, 2, channels, share)
    term_out4 = jnp.stack(
        [
            lax.dot_general(
                hidden[:, f * share : (f + 1) * share], back, contract_rows,
                preferred_element_type=jnp.float32,
            )
            for f in owners
        ]
    ).reshape(2, 2, share, channels)
    spare = -(kernel_term.shape[0] + 1) % 64
    small = jnp.concatenate(
        [kernel_term, term_gain[None], jnp.zeros((spare, channels), jnp.float32)], axis=0
    )
    small4 = jnp.broadcast_to(small, (2, 2) + small.shape)
    stacked = jnp.concatenate(
        [
            (term_in4 * factor).astype(jnp.bfloat16),
            small4.astype(jnp.bfloat16),
            (term_out4 * factor).astype(jnp.bfloat16),
        ],
        axis=2,
    ).reshape(-1, channels)
    chunk = fsdp_summed(stacked)
    first = channels + small.shape[0]
    total = tile_summed(chunk)
    low, high = total[:first], total[first:]
    w_in_grad = low[:channels]
    kernel_grad = low[channels : channels + kernel_term.shape[0]]
    gain_grad = low[channels + kernel_term.shape[0]]
    w_out_grad = high
    return (mixed, field_grad, kernel_grad, gain_grad, w_in_grad, w_out_grad)


def solution(mesh):
    return jax.shard_map(
        body,
        mesh=mesh,
        in_specs=(
            P("fsdp", None, "tile", None),
            P("tile", None),
            P(),
            P(),
            P(None, "fsdp"),
            P("fsdp", None),
            P("fsdp", None, "tile", None),
        ),
        out_specs=(
            P("fsdp", None, "tile", None),
            P("fsdp", None, "tile", None),
            P(),
            P(),
            P(None, "fsdp"),
            P("fsdp", None),
        ),
        check_vma=False,
    )
```

```python
import math

import jax
import jax.numpy as jnp
from jax import lax
from jax.sharding import PartitionSpec as P

eps = 1e-06
inv_root2 = 0.7071067811865476
inv_root_tau = 0.3989422804014327


def extended(cells, sides, width):
    for axis, dim in sides:
        count = lax.axis_size(axis)
        head = lax.slice_in_dim(cells, 0, width, axis=dim)
        tail = lax.slice_in_dim(cells, cells.shape[dim] - width, cells.shape[dim], axis=dim)
        cells = jnp.concatenate(
            [
                lax.ppermute(tail, axis, [(i, (i + 1) % count) for i in range(count)]),
                cells,
                lax.ppermute(head, axis, [((i + 1) % count, i) for i in range(count)]),
            ],
            axis=dim,
        )
    return cells


def exchange(value, axis, bit):
    count = lax.axis_size(axis)
    return lax.ppermute(value, axis, [(i, i ^ (1 << bit)) for i in range(count)])


def fsdp_summed(stacked):
    me = lax.axis_index("fsdp")
    for bit in (0, 1):
        half = stacked.shape[0] // 2
        side = (me >> bit) & 1
        keep = lax.dynamic_slice_in_dim(stacked, side * half, half, 0).astype(jnp.bfloat16)
        send = lax.dynamic_slice_in_dim(stacked, (1 - side) * half, half, 0).astype(jnp.bfloat16)
        got = exchange(send, "fsdp", bit)
        stacked = keep.astype(jnp.float32) + got.astype(jnp.float32)
    return stacked


def tile_summed(chunk):
    assert lax.axis_size("tile") == 64
    me = lax.axis_index("tile")
    groups = ((0, 1), (2, 3), (4, 5))

    def masks(group):
        mine = ((me >> group[0]) & 1) * 2 + ((me >> group[1]) & 1)
        return mine, [(d, ((d >> 1) << group[0]) | ((d & 1) << group[1])) for d in (1, 2, 3)]

    for group in groups[:-1]:
        mine, partners = masks(group)
        size = chunk.shape[0] // 4
        total = lax.dynamic_slice_in_dim(chunk, mine * size, size, 0)
        for d, mask in partners:
            send = lax.dynamic_slice_in_dim(chunk, (mine ^ d) * size, size, 0)
            total = total + swapped(send.astype(jnp.bfloat16), "tile", mask).astype(jnp.float32)
        chunk = total
    mine, partners = masks(groups[-1])
    own = chunk.astype(jnp.bfloat16)
    blocks = jnp.stack([own] + [swapped(own, "tile", mask) for _, mask in partners])
    total = None
    for place in range(4):
        block = lax.dynamic_index_in_dim(blocks, place ^ mine, 0, keepdims=False).astype(jnp.float32)
        total = block if total is None else total + block
    chunk = total.astype(jnp.bfloat16)
    for group in reversed(groups[:-1]):
        mine, partners = masks(group)
        size = chunk.shape[0]
        whole = jnp.zeros((4 * size,) + chunk.shape[1:], chunk.dtype)
        whole = lax.dynamic_update_slice_in_dim(whole, chunk, mine * size, 0)
        for d, mask in partners:
            got = swapped(chunk, "tile", mask)
            whole = lax.dynamic_update_slice_in_dim(whole, got, (mine ^ d) * size, 0)
        chunk = whole
    return chunk.astype(jnp.float32)


def swapped(value, axis, mask):
    count = lax.axis_size(axis)
    return lax.ppermute(value, axis, [(i, i ^ mask) for i in range(count)])


def gathered(shard, anchor, after=None):
    me = lax.axis_index("fsdp")
    high, low = (me >> 1) & 1, me & 1
    if after is not None:
        shard, after = lax.optimization_barrier((shard, after))
    got = exchange(shard, "fsdp", 1)
    pair = jnp.stack([jnp.where(high == 0, shard, got), jnp.where(high == 0, got, shard)])
    pair, anchor = lax.optimization_barrier((pair, anchor))
    other = exchange(pair, "fsdp", 0)
    first, second = jnp.where(low == 0, pair, other), jnp.where(low == 0, other, pair)
    return jnp.stack([first, second], axis=1).reshape((4,) + shard.shape), anchor


def gelu(value):
    return value * 0.5 * (1.0 + lax.erf(value * inv_root2))


def gelu_slope(value):
    return 0.5 * (1.0 + lax.erf(value * inv_root2)) + value * inv_root_tau * jnp.exp(
        -0.5 * value * value
    )


def shift_rows(strip, offset):
    height = strip.shape[1]
    wider = jnp.pad(strip, ((0, 0), (height, height), (0, 0), (0, 0)))
    return lax.dynamic_slice_in_dim(wider, height + offset, height, 1)


def depthwise(padded, kernel):
    height = padded.shape[1] - 6
    width = padded.shape[2] - 6
    total = jnp.zeros((padded.shape[0], height, width, padded.shape[3]), jnp.float32)
    for row in range(7):
        for col in range(7):
            total = (
                total + padded[:, row : row + height, col : col + width, :] * kernel[7 * row + col]
            )
    return total


def body(fields, seam_shift, kernel, gain, w_in, w_out, cotangent):
    height = fields.shape[1]
    width = fields.shape[2]
    channels = fields.shape[3]
    count = fields.shape[0] * height * width
    cells = count * lax.axis_size("tile") * lax.axis_size("fsdp")
    factor = 1.0 / math.sqrt(cells)
    west_shift = seam_shift[0, 0]
    east_shift = seam_shift[0, 1]
    row_pad = ((0, 0), (3, 3), (0, 0), (0, 0))
    widened = extended(fields, (("tile", 2),), 3)
    west = shift_rows(widened[:, :, :3], west_shift)
    east = shift_rows(widened[:, :, width + 3 :], east_shift)
    padded = jnp.pad(jnp.concatenate([west, fields, east], axis=2), row_pad)
    mixed_in = depthwise(padded, kernel)
    rows = mixed_in.reshape(count, channels)
    mean = jnp.mean(rows, axis=-1, keepdims=True)
    centered = rows - mean
    rstd = lax.rsqrt(jnp.mean(centered * centered, axis=-1, keepdims=True) + eps)
    normed = centered * rstd
    scaled = (normed * gain).astype(jnp.bfloat16)
    back = cotangent.reshape(count, channels)
    contract_last = (((1,), (1,)), ((), ()))
    in4, scaled = gathered(w_in, scaled)
    out4, _ = gathered(w_out, back, after=in4)
    full_in = jnp.concatenate([in4[f] for f in range(in4.shape[0])], axis=1)
    full_out = out4.reshape(-1, w_out.shape[1])
    pre = jnp.dot(scaled, full_in, preferred_element_type=jnp.float32)
    hidden = gelu(pre).astype(jnp.bfloat16)
    branch = jnp.dot(hidden, full_out, preferred_element_type=jnp.float32)
    d_hidden = lax.dot_general(back, full_out, contract_last, preferred_element_type=jnp.float32)
    residual = fields.reshape(count, channels).astype(jnp.float32)
    mixed = (residual + branch).astype(jnp.bfloat16).reshape(fields.shape)
    d_pre = (d_hidden * gelu_slope(pre)).astype(jnp.bfloat16)
    d_scaled = lax.dot_general(d_pre, full_in, contract_last, preferred_element_type=jnp.float32)
    term_gain = jnp.sum(d_scaled * normed, axis=0) * factor
    d_normed = d_scaled * gain
    d_rows = (
        d_normed
        - jnp.mean(d_normed, axis=-1, keepdims=True)
        - normed * jnp.mean(d_normed * normed, axis=-1, keepdims=True)
    ) * rstd
    d_mixed = d_rows.reshape(mixed_in.shape)
    unused, pullback = jax.vjp(depthwise, padded.astype(jnp.float32), kernel)
    d_padded, kernel_term = pullback(d_mixed)
    kernel_term = kernel_term * factor
    d_core = d_padded[:, 3 : height + 3]
    d_west = shift_rows(d_core[:, :, :3], -west_shift)
    d_east = shift_rows(d_core[:, :, width + 3 :], -east_shift)
    returned = extended(
        jnp.concatenate([d_west, d_east], axis=2).astype(jnp.bfloat16), (("tile", 2),), 3
    ).astype(jnp.float32)
    own = cotangent.astype(jnp.float32) + d_core[:, :, 3 : width + 3]
    field_grad = jnp.concatenate(
        [
            own[:, :, :3] + returned[:, :, :3],
            own[:, :, 3 : width - 3],
            own[:, :, width - 3 :] + returned[:, :, 9:],
        ],
        axis=2,
    ).astype(jnp.bfloat16)
    parts = lax.axis_size("fsdp")
    assert parts == 4
    share = full_in.shape[1] // parts
    owners = [0, 2, 1, 3]
    contract_rows = (((0,), (0,)), ((), ()))
    term_in4 = jnp.stack(
        [
            lax.dot_general(
                scaled, d_pre[:, f * share : (f + 1) * share], contract_rows,
                preferred_element_type=jnp.float32,
            )
            for f in owners
        ]
    ).reshape(2, 2, channels, share)
    term_out4 = jnp.stack(
        [
            lax.dot_general(
                hidden[:, f * share : (f + 1) * share], back, contract_rows,
                preferred_element_type=jnp.float32,
            )
            for f in owners
        ]
    ).reshape(2, 2, share, channels)
    spare = -(kernel_term.shape[0] + 1) % 64
    small = jnp.concatenate(
        [kernel_term, term_gain[None], jnp.zeros((spare, channels), jnp.float32)], axis=0
    )
    small4 = jnp.broadcast_to(small, (2, 2) + small.shape)
    stacked = jnp.concatenate(
        [
            (term_in4 * factor).astype(jnp.bfloat16),
            small4.astype(jnp.bfloat16),
            (term_out4 * factor).astype(jnp.bfloat16),
        ],
        axis=2,
    ).reshape(-1, channels)
    chunk = fsdp_summed(stacked)
    first = channels + small.shape[0]
    total = tile_summed(chunk)
    low, high = total[:first], total[first:]
    w_in_grad = low[:channels]
    kernel_grad = low[channels : channels + kernel_term.shape[0]]
    gain_grad = low[channels + kernel_term.shape[0]]
    w_out_grad = high
    return (mixed, field_grad, kernel_grad, gain_grad, w_in_grad, w_out_grad)


def solution(mesh):
    return jax.shard_map(
        body,
        mesh=mesh,
        in_specs=(
            P("fsdp", None, "tile", None),
            P("tile", None),
            P(),
            P(),
            P(None, "fsdp"),
            P("fsdp", None),
            P("fsdp", None, "tile", None),
        ),
        out_specs=(
            P("fsdp", None, "tile", None),
            P("fsdp", None, "tile", None),
            P(),
            P(),
            P(None, "fsdp"),
            P("fsdp", None),
        ),
        check_vma=False,
    )
```

```python
import math

import jax
import jax.numpy as jnp
from jax import lax
from jax.sharding import PartitionSpec as P

eps = 1e-06
inv_root2 = 0.7071067811865476
inv_root_tau = 0.3989422804014327


def extended(cells, sides, width):
    for axis, dim in sides:
        count = lax.axis_size(axis)
        head = lax.slice_in_dim(cells, 0, width, axis=dim)
        tail = lax.slice_in_dim(cells, cells.shape[dim] - width, cells.shape[dim], axis=dim)
        cells = jnp.concatenate(
            [
                lax.ppermute(tail, axis, [(i, (i + 1) % count) for i in range(count)]),
                cells,
                lax.ppermute(head, axis, [((i + 1) % count, i) for i in range(count)]),
            ],
            axis=dim,
        )
    return cells


def exchange(value, axis, bit):
    count = lax.axis_size(axis)
    return lax.ppermute(value, axis, [(i, i ^ (1 << bit)) for i in range(count)])


def fsdp_summed(stacked, anchor):
    me = lax.axis_index("fsdp")
    for bit in (0, 1):
        half = stacked.shape[0] // 2
        side = (me >> bit) & 1
        keep = lax.dynamic_slice_in_dim(stacked, side * half, half, 0).astype(jnp.bfloat16)
        send = lax.dynamic_slice_in_dim(stacked, (1 - side) * half, half, 0).astype(jnp.bfloat16)
        got = exchange(send, "fsdp", bit)
        stacked = keep.astype(jnp.float32) + got.astype(jnp.float32)
        if bit == 0:
            stacked, anchor = lax.optimization_barrier((stacked, anchor))
    return stacked, anchor


def fsdp_everywhere(small):
    me = lax.axis_index("fsdp")
    own = small.astype(jnp.bfloat16)
    blocks = jnp.stack([own] + [swapped(own, "fsdp", d) for d in (1, 2, 3)])
    total = None
    for place in range(4):
        block = lax.dynamic_index_in_dim(blocks, place ^ me, 0, keepdims=False)
        block = block.astype(jnp.float32)
        total = block if total is None else total + block
    return total


def tile_summed(chunk):
    assert lax.axis_size("tile") == 64
    me = lax.axis_index("tile")
    groups = ((0, 1), (2, 3), (4, 5))

    def masks(group):
        mine = ((me >> group[0]) & 1) * 2 + ((me >> group[1]) & 1)
        return mine, [(d, ((d >> 1) << group[0]) | ((d & 1) << group[1])) for d in (1, 2, 3)]

    for group in groups[:-1]:
        mine, partners = masks(group)
        size = chunk.shape[0] // 4
        total = lax.dynamic_slice_in_dim(chunk, mine * size, size, 0)
        for d, mask in partners:
            send = lax.dynamic_slice_in_dim(chunk, (mine ^ d) * size, size, 0)
            total = total + swapped(send.astype(jnp.bfloat16), "tile", mask).astype(jnp.float32)
        chunk = total
    mine, partners = masks(groups[-1])
    own = chunk.astype(jnp.bfloat16)
    blocks = jnp.stack([own] + [swapped(own, "tile", mask) for _, mask in partners])
    total = None
    for place in range(4):
        block = lax.dynamic_index_in_dim(blocks, place ^ mine, 0, keepdims=False).astype(jnp.float32)
        total = block if total is None else total + block
    chunk = total.astype(jnp.bfloat16)
    for group in reversed(groups[:-1]):
        mine, partners = masks(group)
        size = chunk.shape[0]
        whole = jnp.zeros((4 * size,) + chunk.shape[1:], chunk.dtype)
        whole = lax.dynamic_update_slice_in_dim(whole, chunk, mine * size, 0)
        for d, mask in partners:
            got = swapped(chunk, "tile", mask)
            whole = lax.dynamic_update_slice_in_dim(whole, got, (mine ^ d) * size, 0)
        chunk = whole
    return chunk.astype(jnp.float32)


def swapped(value, axis, mask):
    count = lax.axis_size(axis)
    return lax.ppermute(value, axis, [(i, i ^ mask) for i in range(count)])


def gathered(shard, anchor):
    me = lax.axis_index("fsdp")
    high, low = (me >> 1) & 1, me & 1
    got = exchange(shard, "fsdp", 1)
    pair = jnp.stack([jnp.where(high == 0, shard, got), jnp.where(high == 0, got, shard)])
    pair, anchor = lax.optimization_barrier((pair, anchor))
    other = exchange(pair, "fsdp", 0)
    first, second = jnp.where(low == 0, pair, other), jnp.where(low == 0, other, pair)
    return jnp.stack([first, second], axis=1).reshape((4,) + shard.shape), anchor


def gelu(value):
    return value * 0.5 * (1.0 + lax.erf(value * inv_root2))


def gelu_slope(value):
    return 0.5 * (1.0 + lax.erf(value * inv_root2)) + value * inv_root_tau * jnp.exp(
        -0.5 * value * value
    )


def shift_rows(strip, offset):
    height = strip.shape[1]
    wider = jnp.pad(strip, ((0, 0), (height, height), (0, 0), (0, 0)))
    return lax.dynamic_slice_in_dim(wider, height + offset, height, 1)


def depthwise(padded, kernel):
    height = padded.shape[1] - 6
    width = padded.shape[2] - 6
    total = jnp.zeros((padded.shape[0], height, width, padded.shape[3]), jnp.float32)
    for row in range(7):
        for col in range(7):
            total = (
                total + padded[:, row : row + height, col : col + width, :] * kernel[7 * row + col]
            )
    return total


def body(fields, seam_shift, kernel, gain, w_in, w_out, cotangent):
    height = fields.shape[1]
    width = fields.shape[2]
    channels = fields.shape[3]
    count = fields.shape[0] * height * width
    cells = count * lax.axis_size("tile") * lax.axis_size("fsdp")
    factor = 1.0 / math.sqrt(cells)
    west_shift = seam_shift[0, 0]
    east_shift = seam_shift[0, 1]
    row_pad = ((0, 0), (3, 3), (0, 0), (0, 0))
    widened = extended(fields, (("tile", 2),), 3)
    west = shift_rows(widened[:, :, :3], west_shift)
    east = shift_rows(widened[:, :, width + 3 :], east_shift)
    padded = jnp.pad(jnp.concatenate([west, fields, east], axis=2), row_pad)
    mixed_in = depthwise(padded, kernel)
    rows = mixed_in.reshape(count, channels)
    mean = jnp.mean(rows, axis=-1, keepdims=True)
    centered = rows - mean
    rstd = lax.rsqrt(jnp.mean(centered * centered, axis=-1, keepdims=True) + eps)
    normed = centered * rstd
    scaled = (normed * gain).astype(jnp.bfloat16)
    back = cotangent.reshape(count, channels)
    contract_last = (((1,), (1,)), ((), ()))
    both, scaled = gathered(jnp.stack([w_in, w_out]), scaled)
    full_in = jnp.concatenate([both[f, 0] for f in range(both.shape[0])], axis=1)
    full_out = both[:, 1].reshape(-1, w_out.shape[1])
    pre = jnp.dot(scaled, full_in, preferred_element_type=jnp.float32)
    hidden = gelu(pre).astype(jnp.bfloat16)
    branch = jnp.dot(hidden, full_out, preferred_element_type=jnp.float32)
    d_hidden = lax.dot_general(back, full_out, contract_last, preferred_element_type=jnp.float32)
    residual = fields.reshape(count, channels).astype(jnp.float32)
    mixed = (residual + branch).astype(jnp.bfloat16).reshape(fields.shape)
    d_pre = (d_hidden * gelu_slope(pre)).astype(jnp.bfloat16)
    d_scaled = lax.dot_general(d_pre, full_in, contract_last, preferred_element_type=jnp.float32)
    parts = lax.axis_size("fsdp")
    assert parts == 4
    share = full_in.shape[1] // parts
    owners = [0, 2, 1, 3]
    contract_rows = (((0,), (0,)), ((), ()))
    term_in4 = jnp.stack(
        [
            lax.dot_general(
                scaled, d_pre[:, f * share : (f + 1) * share], contract_rows,
                preferred_element_type=jnp.float32,
            )
            for f in owners
        ]
    ).reshape(2, 2, channels, share)
    term_out4 = jnp.stack(
        [
            lax.dot_general(
                hidden[:, f * share : (f + 1) * share], back, contract_rows,
                preferred_element_type=jnp.float32,
            )
            for f in owners
        ]
    ).reshape(2, 2, share, channels)
    stacked = jnp.concatenate(
        [(term_in4 * factor).astype(jnp.bfloat16), (term_out4 * factor).astype(jnp.bfloat16)],
        axis=2,
    ).reshape(-1, channels)
    chunk, d_scaled = fsdp_summed(stacked, d_scaled)
    term_gain = jnp.sum(d_scaled * normed, axis=0) * factor
    d_normed = d_scaled * gain
    d_rows = (
        d_normed
        - jnp.mean(d_normed, axis=-1, keepdims=True)
        - normed * jnp.mean(d_normed * normed, axis=-1, keepdims=True)
    ) * rstd
    d_mixed = d_rows.reshape(mixed_in.shape)
    unused, pullback = jax.vjp(depthwise, padded.astype(jnp.float32), kernel)
    d_padded, kernel_term = pullback(d_mixed)
    kernel_term = kernel_term * factor
    d_core = d_padded[:, 3 : height + 3]
    d_west = shift_rows(d_core[:, :, :3], -west_shift)
    d_east = shift_rows(d_core[:, :, width + 3 :], -east_shift)
    returned = extended(
        jnp.concatenate([d_west, d_east], axis=2).astype(jnp.bfloat16), (("tile", 2),), 3
    ).astype(jnp.float32)
    own = cotangent.astype(jnp.float32) + d_core[:, :, 3 : width + 3]
    field_grad = jnp.concatenate(
        [
            own[:, :, :3] + returned[:, :, :3],
            own[:, :, 3 : width - 3],
            own[:, :, width - 3 :] + returned[:, :, 9:],
        ],
        axis=2,
    ).astype(jnp.bfloat16)
    spare = -(kernel_term.shape[0] + 1) % 64
    small = jnp.concatenate(
        [kernel_term, term_gain[None], jnp.zeros((spare, channels), jnp.float32)], axis=0
    )
    total = tile_summed(jnp.concatenate([chunk, fsdp_everywhere(small)], axis=0))
    w_in_grad = total[:channels]
    w_out_grad = total[channels : 2 * channels]
    kernel_grad = total[2 * channels : 2 * channels + kernel_term.shape[0]]
    gain_grad = total[2 * channels + kernel_term.shape[0]]
    return (mixed, field_grad, kernel_grad, gain_grad, w_in_grad, w_out_grad)


def solution(mesh):
    return jax.shard_map(
        body,
        mesh=mesh,
        in_specs=(
            P("fsdp", None, "tile", None),
            P("tile", None),
            P(),
            P(),
            P(None, "fsdp"),
            P("fsdp", None),
            P("fsdp", None, "tile", None),
        ),
        out_specs=(
            P("fsdp", None, "tile", None),
            P("fsdp", None, "tile", None),
            P(),
            P(),
            P(None, "fsdp"),
            P("fsdp", None),
        ),
        check_vma=False,
    )
```

```python
import math

import jax
import jax.numpy as jnp
from jax import lax
from jax.sharding import PartitionSpec as P

eps = 1e-06
inv_root2 = 0.7071067811865476
inv_root_tau = 0.3989422804014327


def extended(cells, sides, width):
    for axis, dim in sides:
        count = lax.axis_size(axis)
        head = lax.slice_in_dim(cells, 0, width, axis=dim)
        tail = lax.slice_in_dim(cells, cells.shape[dim] - width, cells.shape[dim], axis=dim)
        cells = jnp.concatenate(
            [
                lax.ppermute(tail, axis, [(i, (i + 1) % count) for i in range(count)]),
                cells,
                lax.ppermute(head, axis, [((i + 1) % count, i) for i in range(count)]),
            ],
            axis=dim,
        )
    return cells


def exchange(value, axis, bit):
    count = lax.axis_size(axis)
    return lax.ppermute(value, axis, [(i, i ^ (1 << bit)) for i in range(count)])


def fsdp_summed(stacked):
    me = lax.axis_index("fsdp")
    for bit in (0, 1):
        half = stacked.shape[0] // 2
        side = (me >> bit) & 1
        keep = lax.dynamic_slice_in_dim(stacked, side * half, half, 0).astype(jnp.bfloat16)
        send = lax.dynamic_slice_in_dim(stacked, (1 - side) * half, half, 0).astype(jnp.bfloat16)
        got = exchange(send, "fsdp", bit)
        stacked = keep.astype(jnp.float32) + got.astype(jnp.float32)
    return stacked


def tile_summed(chunk):
    assert lax.axis_size("tile") == 64
    me = lax.axis_index("tile")
    groups = ((2, 3), (0, 1), (4, 5))

    def masks(group):
        mine = ((me >> group[0]) & 1) * 2 + ((me >> group[1]) & 1)
        return mine, [(d, ((d >> 1) << group[0]) | ((d & 1) << group[1])) for d in (1, 2, 3)]

    for group in groups[:-1]:
        mine, partners = masks(group)
        size = chunk.shape[0] // 4
        total = lax.dynamic_slice_in_dim(chunk, mine * size, size, 0)
        for d, mask in partners:
            send = lax.dynamic_slice_in_dim(chunk, (mine ^ d) * size, size, 0)
            total = total + swapped(send.astype(jnp.bfloat16), "tile", mask).astype(jnp.float32)
        chunk = total
    mine, partners = masks(groups[-1])
    own = chunk.astype(jnp.bfloat16)
    blocks = jnp.stack([own] + [swapped(own, "tile", mask) for _, mask in partners])
    total = None
    for place in range(4):
        block = lax.dynamic_index_in_dim(blocks, place ^ mine, 0, keepdims=False).astype(jnp.float32)
        total = block if total is None else total + block
    chunk = total.astype(jnp.bfloat16)
    for group in reversed(groups[:-1]):
        mine, partners = masks(group)
        size = chunk.shape[0]
        whole = jnp.zeros((4 * size,) + chunk.shape[1:], chunk.dtype)
        whole = lax.dynamic_update_slice_in_dim(whole, chunk, mine * size, 0)
        for d, mask in partners:
            got = swapped(chunk, "tile", mask)
            whole = lax.dynamic_update_slice_in_dim(whole, got, (mine ^ d) * size, 0)
        chunk = whole
    return chunk.astype(jnp.float32)


def swapped(value, axis, mask):
    count = lax.axis_size(axis)
    return lax.ppermute(value, axis, [(i, i ^ mask) for i in range(count)])


def gathered(shard, anchor):
    me = lax.axis_index("fsdp")
    high, low = (me >> 1) & 1, me & 1
    got = exchange(shard, "fsdp", 1)
    pair = jnp.stack([jnp.where(high == 0, shard, got), jnp.where(high == 0, got, shard)])
    pair, anchor = lax.optimization_barrier((pair, anchor))
    other = exchange(pair, "fsdp", 0)
    first, second = jnp.where(low == 0, pair, other), jnp.where(low == 0, other, pair)
    return jnp.stack([first, second], axis=1).reshape((4,) + shard.shape), anchor


def gelu(value):
    return value * 0.5 * (1.0 + lax.erf(value * inv_root2))


def gelu_slope(value):
    return 0.5 * (1.0 + lax.erf(value * inv_root2)) + value * inv_root_tau * jnp.exp(
        -0.5 * value * value
    )


def shift_rows(strip, offset):
    height = strip.shape[1]
    wider = jnp.pad(strip, ((0, 0), (height, height), (0, 0), (0, 0)))
    return lax.dynamic_slice_in_dim(wider, height + offset, height, 1)


def depthwise(padded, kernel):
    height = padded.shape[1] - 6
    width = padded.shape[2] - 6
    total = jnp.zeros((padded.shape[0], height, width, padded.shape[3]), jnp.float32)
    for row in range(7):
        for col in range(7):
            total = (
                total + padded[:, row : row + height, col : col + width, :] * kernel[7 * row + col]
            )
    return total


def body(fields, seam_shift, kernel, gain, w_in, w_out, cotangent):
    height = fields.shape[1]
    width = fields.shape[2]
    channels = fields.shape[3]
    count = fields.shape[0] * height * width
    cells = count * lax.axis_size("tile") * lax.axis_size("fsdp")
    factor = 1.0 / math.sqrt(cells)
    west_shift = seam_shift[0, 0]
    east_shift = seam_shift[0, 1]
    row_pad = ((0, 0), (3, 3), (0, 0), (0, 0))
    widened = extended(fields, (("tile", 2),), 3)
    west = shift_rows(widened[:, :, :3], west_shift)
    east = shift_rows(widened[:, :, width + 3 :], east_shift)
    padded = jnp.pad(jnp.concatenate([west, fields, east], axis=2), row_pad)
    mixed_in = depthwise(padded, kernel)
    rows = mixed_in.reshape(count, channels)
    mean = jnp.mean(rows, axis=-1, keepdims=True)
    centered = rows - mean
    rstd = lax.rsqrt(jnp.mean(centered * centered, axis=-1, keepdims=True) + eps)
    normed = centered * rstd
    scaled = (normed * gain).astype(jnp.bfloat16)
    back = cotangent.reshape(count, channels)
    contract_last = (((1,), (1,)), ((), ()))
    both, scaled = gathered(jnp.stack([w_in, w_out]), scaled)
    full_in = jnp.concatenate([both[f, 0] for f in range(both.shape[0])], axis=1)
    full_out = both[:, 1].reshape(-1, w_out.shape[1])
    pre = jnp.dot(scaled, full_in, preferred_element_type=jnp.float32)
    hidden = gelu(pre).astype(jnp.bfloat16)
    branch = jnp.dot(hidden, full_out, preferred_element_type=jnp.float32)
    d_hidden = lax.dot_general(back, full_out, contract_last, preferred_element_type=jnp.float32)
    residual = fields.reshape(count, channels).astype(jnp.float32)
    mixed = (residual + branch).astype(jnp.bfloat16).reshape(fields.shape)
    d_pre = (d_hidden * gelu_slope(pre)).astype(jnp.bfloat16)
    d_scaled = lax.dot_general(d_pre, full_in, contract_last, preferred_element_type=jnp.float32)
    term_gain = jnp.sum(d_scaled * normed, axis=0) * factor
    d_normed = d_scaled * gain
    d_rows = (
        d_normed
        - jnp.mean(d_normed, axis=-1, keepdims=True)
        - normed * jnp.mean(d_normed * normed, axis=-1, keepdims=True)
    ) * rstd
    d_mixed = d_rows.reshape(mixed_in.shape)
    unused, pullback = jax.vjp(depthwise, padded.astype(jnp.float32), kernel)
    d_padded, kernel_term = pullback(d_mixed)
    kernel_term = kernel_term * factor
    d_core = d_padded[:, 3 : height + 3]
    d_west = shift_rows(d_core[:, :, :3], -west_shift)
    d_east = shift_rows(d_core[:, :, width + 3 :], -east_shift)
    returned = extended(
        jnp.concatenate([d_west, d_east], axis=2).astype(jnp.bfloat16), (("tile", 2),), 3
    ).astype(jnp.float32)
    own = cotangent.astype(jnp.float32) + d_core[:, :, 3 : width + 3]
    field_grad = jnp.concatenate(
        [
            own[:, :, :3] + returned[:, :, :3],
            own[:, :, 3 : width - 3],
            own[:, :, width - 3 :] + returned[:, :, 9:],
        ],
        axis=2,
    ).astype(jnp.bfloat16)
    parts = lax.axis_size("fsdp")
    assert parts == 4
    share = full_in.shape[1] // parts
    owners = [0, 2, 1, 3]
    contract_rows = (((0,), (0,)), ((), ()))
    term_in4 = jnp.stack(
        [
            lax.dot_general(
                scaled, d_pre[:, f * share : (f + 1) * share], contract_rows,
                preferred_element_type=jnp.float32,
            )
            for f in owners
        ]
    ).reshape(2, 2, channels, share)
    term_out4 = jnp.stack(
        [
            lax.dot_general(
                hidden[:, f * share : (f + 1) * share], back, contract_rows,
                preferred_element_type=jnp.float32,
            )
            for f in owners
        ]
    ).reshape(2, 2, share, channels)
    spare = -(kernel_term.shape[0] + 1) % 64
    small = jnp.concatenate(
        [kernel_term, term_gain[None], jnp.zeros((spare, channels), jnp.float32)], axis=0
    )
    small4 = jnp.broadcast_to(small, (2, 2) + small.shape)
    stacked = jnp.concatenate(
        [
            (term_in4 * factor).astype(jnp.bfloat16),
            small4.astype(jnp.bfloat16),
            (term_out4 * factor).astype(jnp.bfloat16),
        ],
        axis=2,
    ).reshape(-1, channels)
    chunk = fsdp_summed(stacked)
    first = channels + small.shape[0]
    total = tile_summed(chunk)
    low, high = total[:first], total[first:]
    w_in_grad = low[:channels]
    kernel_grad = low[channels : channels + kernel_term.shape[0]]
    gain_grad = low[channels + kernel_term.shape[0]]
    w_out_grad = high
    return (mixed, field_grad, kernel_grad, gain_grad, w_in_grad, w_out_grad)


def solution(mesh):
    return jax.shard_map(
        body,
        mesh=mesh,
        in_specs=(
            P("fsdp", None, "tile", None),
            P("tile", None),
            P(),
            P(),
            P(None, "fsdp"),
            P("fsdp", None),
            P("fsdp", None, "tile", None),
        ),
        out_specs=(
            P("fsdp", None, "tile", None),
            P("fsdp", None, "tile", None),
            P(),
            P(),
            P(None, "fsdp"),
            P("fsdp", None),
        ),
        check_vma=False,
    )
```
